32 devices in a mesh: rot: 16 (over z, x, core), term: 2 (over y).
Axes of the slice: x: 2, y: 2, z: 4, core: 2. Of those that a mesh axis runs over, the one named last changes fastest.
Arguments:
- receptor_grids: bfloat16 [22, 128, 1024], P('term', 'rot'), may hold values from -6 to 6
- term_weights: float32 [22], P('term'), may hold values from 0.5 to 2
- atom_weights: float32 [22, 256], P('term'), may hold values from -0.125 to 0.125
- ligand_cells: int32 [3, 32, 256], P(None, 'rot'), may hold values from 0 to 15
Outputs:
- best_scores: float32 [4, 32], P(None, 'rot')
- best_overall: float32 [4], replicated
The draws below stay inside these ranges and needn't reach their ends.
All inputs are finite; a program needn't handle non-finite values.
Results may differ from the reference program's by a relative error of at most 0.0017.
Values may be sent and summed in bfloat16 or wider, within the bound.
No kernel may reach another device: no remote copies, remote signals or barrier semaphores. Data moves between devices by JAX's collectives and lax.ppermute only.
A program may use at most 128 MiB of HBM per device.

```python
import jax
import jax.numpy as jnp
from jax import lax

G = 32
TERMS = 22
REC = 4
ATOMS = 256
LB = 16
ROTS = 32


def touch_ends(drawn, rng, smallest, high):
    spot = [jax.random.randint(jax.random.fold_in(rng, axis), (), 0, length) for axis, length in enumerate(drawn.shape)]
    widest = drawn.shape.index(max(drawn.shape))
    next_to = spot[:widest] + [(spot[widest] + 1) % drawn.shape[widest]] + spot[widest + 1:]
    return drawn.at[tuple(spot)].set(smallest).at[tuple(next_to)].set(high)


def block_levels(stream_key, shape, pieces, least, high):
    def one(position, shards_of):
        draws = jax.random.uniform(jax.random.fold_in(jax.random.fold_in(stream_key, 6), position), (shards_of,), jnp.float32, least / len(pieces), high / len(pieces))
        return jnp.repeat(jnp.exp(draws), shape[position] // shards_of).reshape((-1,) + (1,) * (len(shape) - position - 1))

    gain = one(*pieces[0])
    for cut in pieces[1:]:
        gain = gain * one(*cut)
    return gain


def gaussian(key, extent, deviation, most, split=(), held_as=jnp.bfloat16):
    loudness = block_levels(key, extent, split, -0.22, 0.18) if split else 1.0
    result = jax.random.normal(key, extent, jnp.float32) * deviation * loudness
    return jnp.minimum(jnp.maximum(result, -most), most).astype(held_as)


def setup_inputs(seed: int = 0) -> dict:
    streams_of = jax.random.split(jax.random.key(seed), 5)
    receptor_grids = gaussian(streams_of[0], (TERMS, REC * G, G * G), 1.0, 6.0, ((0, 2), (1, 16)))
    term_weights = jnp.clip(0.5 + 1.5 * jax.random.uniform(streams_of[1], (TERMS,), jnp.float32) ** block_levels(streams_of[1], (TERMS,), ((0, 2),), -0.2, 0.2), 0.5, 2.0)
    atom_weights = gaussian(streams_of[2], (TERMS, ATOMS), (ATOMS * 8) ** -0.5, 0.125, ((0, 2),), jnp.float32)
    ligand_cells = touch_ends(jax.random.randint(streams_of[3], (3, ROTS, ATOMS), 0, LB), jax.random.fold_in(streams_of[3], 1), 0, LB - 1).astype(jnp.int32)
    return dict(receptor_grids=receptor_grids, term_weights=term_weights, atom_weights=atom_weights, ligand_cells=ligand_cells)


def reference(receptor_grids, term_weights, atom_weights, ligand_cells):
    grid_data = receptor_grids.astype(jnp.float32).reshape(TERMS, REC, G, G, G)
    rec_spec = jnp.fft.rfftn(grid_data, axes=(2, 3, 4))
    weighted = rec_spec * term_weights[:, None, None, None, None]

    def per_rotation(voxels):
        flat_index = (voxels[0] * LB + voxels[1]) * LB + voxels[2]
        summed = jax.ops.segment_sum(atom_weights.T, flat_index, num_segments=LB ** 3)
        box_grid = summed.T.reshape(TERMS, LB, LB, LB)
        padded = jnp.zeros((TERMS, G, G, G), box_grid.dtype).at[:, :LB, :LB, :LB].set(box_grid)
        lig_spec = jnp.fft.rfftn(padded, axes=(1, 2, 3))
        products = jnp.sum(jnp.conj(lig_spec)[:, None] * weighted, axis=0)
        scores = jnp.fft.irfftn(products, s=(G, G, G), axes=(1, 2, 3))
        return jnp.max(scores.reshape(REC, G * G * G), axis=1)

    best_scores = lax.map(per_rotation, jnp.moveaxis(ligand_cells, 1, 0)).T
    return best_scores, jnp.max(best_scores, axis=1)
```

```python
import math

import numpy as np

import jax
import jax.numpy as jnp
from jax import lax
from jax.sharding import PartitionSpec as P

G = 32
HZ = G // 2 + 1
LB = 16

HIGH = lax.Precision.HIGH
HIGHEST = lax.Precision.HIGHEST


def line_table(freq_count, cell_count):
    freq = np.arange(freq_count)[:, None]
    cell = np.arange(cell_count)[None, :]
    phase = (freq * cell % G).astype(np.float64) * (2.0 * math.pi / G)
    return np.cos(phase).astype(np.float32), np.sin(phase).astype(np.float32)


def plane_tables(side):
    cy, sy = line_table(G, side)
    cz, sz = line_table(HZ, side)
    cy = jnp.asarray(cy.T)[:, None, :, None]
    sy = jnp.asarray(sy.T)[:, None, :, None]
    cz = jnp.asarray(cz.T)[None, :, None, :]
    sz = jnp.asarray(sz.T)[None, :, None, :]
    cos_t = (cy * cz - sy * sz).reshape(side * side, G * HZ)
    sin_t = (sy * cz + cy * sz).reshape(side * side, G * HZ)
    return cos_t, sin_t


def split_bf16(table):
    upper = table.astype(jnp.bfloat16)
    lower = (table - upper.astype(jnp.float32)).astype(jnp.bfloat16)
    return upper, lower


def mix_table(cell_count):
    cos_x, sin_x = line_table(G, cell_count)
    return jnp.asarray(np.concatenate([cos_x, sin_x], axis=0))


def dot2(rows, upper, lower):
    first = jnp.dot(rows, upper, preferred_element_type=jnp.float32)
    second = jnp.dot(rows, lower, preferred_element_type=jnp.float32)
    return first + second


def receptor_spectra(grids, cos_hi, cos_lo, sin_hi, sin_lo):
    terms, rows, cells = grids.shape
    receptors = rows // G
    flat = grids.reshape(terms * rows, cells)
    plane_re = dot2(flat, cos_hi, cos_lo).reshape(terms, receptors, G, G * HZ)
    plane_ims = dot2(flat, sin_hi, sin_lo).reshape(terms, receptors, G, G * HZ)
    mix = mix_table(G)
    mixed_re = jnp.einsum("px,trxq->trpq", mix, plane_re, precision=HIGH)
    mixed_ims = jnp.einsum("px,trxq->trpq", mix, plane_ims, precision=HIGH)
    spec_re = mixed_re[:, :, :G] - mixed_ims[:, :, G:]
    spec_im = -mixed_ims[:, :, :G] - mixed_re[:, :, G:]
    return spec_re, spec_im


def ligand_spectra(voxels, coefficients, box_cos, box_sin):
    rot_count = voxels.shape[1]
    terms = coefficients.shape[0]
    flat_index = (voxels[0] * LB + voxels[1]) * LB + voxels[2]
    cells = jnp.arange(LB**3, dtype=jnp.int32)
    onehot = (flat_index[:, :, None] == cells[None, None, :]).astype(jnp.float32)
    grid = jnp.einsum("ta,nac->tnc", coefficients, onehot, precision=HIGHEST)
    grid = grid.reshape(terms, rot_count, LB, LB * LB)
    plane_re = jnp.einsum("tnxc,cq->tnxq", grid, box_cos, precision=HIGH)
    plane_ims = jnp.einsum("tnxc,cq->tnxq", grid, box_sin, precision=HIGH)
    mix = mix_table(LB)
    mixed_re = jnp.einsum("px,tnxq->tnpq", mix, plane_re, precision=HIGH)
    mixed_ims = jnp.einsum("px,tnxq->tnpq", mix, plane_ims, precision=HIGH)
    lig_re = mixed_re[:, :, :G] - mixed_ims[:, :, G:]
    lig_im = -mixed_ims[:, :, :G] - mixed_re[:, :, G:]
    return lig_re, lig_im


def correlate(lig_re, lig_im, rec_re, rec_im):
    lr = lig_re[:, None]
    li = lig_im[:, None]
    rr = rec_re[:, :, None]
    ri = rec_im[:, :, None]
    prod_re = jnp.sum(lr * rr + li * ri, axis=0)
    prod_im = jnp.sum(lr * ri - li * rr, axis=0)
    return jnp.stack([prod_re, prod_im], axis=0)


def inverse_scores(products, cos_t, sin_t):
    mix = mix_table(G)
    mixed = jnp.einsum("xp,srnpq->srnxq", mix, products, precision=HIGH)
    inv_re = mixed[0, :, :, :G] - mixed[1, :, :, G:]
    inv_im = mixed[1, :, :, :G] + mixed[0, :, :, G:]
    freq_z = np.arange(G * HZ) % HZ
    fold = np.where((freq_z == 0) | (freq_z == G // 2), 1.0, 2.0) / float(G**3)
    fold = jnp.asarray(fold.astype(np.float32))
    scores = jnp.einsum("rnxq,cq->rnxc", inv_re * fold, cos_t, precision=HIGH)
    scores = scores - jnp.einsum("rnxq,cq->rnxc", inv_im * fold, sin_t, precision=HIGH)
    return scores


def body(receptor_grids, term_weights, atom_weights, ligand_cells):
    gathered = lax.all_gather(receptor_grids, "rot", axis=1, tiled=True)
    with jax.named_scope("twiddle_tables"):
        cos_t, sin_t = plane_tables(G)
        box_cos, box_sin = plane_tables(LB)
        cos_hi, cos_lo = split_bf16(cos_t)
        sin_hi, sin_lo = split_bf16(sin_t)
        tables = lax.optimization_barrier(
            (cos_t, sin_t, box_cos, box_sin, cos_hi, cos_lo, sin_hi, sin_lo)
        )
        cos_t, sin_t, box_cos, box_sin, cos_hi, cos_lo, sin_hi, sin_lo = tables
    with jax.named_scope("ligand_spectra"):
        coefficients = atom_weights * term_weights[:, None]
        lig_re, lig_im = ligand_spectra(ligand_cells, coefficients, box_cos, box_sin)
    with jax.named_scope("receptor_spectra"):
        rec_re, rec_im = receptor_spectra(gathered, cos_hi, cos_lo, sin_hi, sin_lo)
    with jax.named_scope("correlate"):
        products = correlate(lig_re, lig_im, rec_re, rec_im)
    products = lax.psum_scatter(products, "term", scatter_dimension=2, tiled=True)
    with jax.named_scope("inverse_scores"):
        scores = inverse_scores(products, cos_t, sin_t)
        best_here = jnp.max(scores, axis=(2, 3))
    best_all = lax.all_gather(best_here, ("rot", "term"), axis=1, tiled=True)
    rot_local = ligand_cells.shape[1]
    start = lax.axis_index("rot") * rot_local
    best_scores = lax.dynamic_slice_in_dim(best_all, start, rot_local, axis=1)
    best_overall = jnp.max(best_all, axis=1)
    return (best_scores, best_overall)


def solution(mesh):
    placed = (P("term", "rot", None), P("term"), P("term", None), P(None, "rot", None))
    return jax.shard_map(
        body, mesh=mesh, in_specs=placed, out_specs=(P(None, "rot"), P()), check_vma=False
    )
```

```python
import math

import numpy as np

import jax
import jax.numpy as jnp
from jax import lax
from jax.sharding import PartitionSpec as P

G = 32
HZ = G // 2 + 1
LB = 16

HIGH = lax.Precision.HIGH
HIGHEST = lax.Precision.HIGHEST


def line_table(freq_count, cell_count):
    freq = np.arange(freq_count)[:, None]
    cell = np.arange(cell_count)[None, :]
    phase = (freq * cell % G).astype(np.float64) * (2.0 * math.pi / G)
    return np.cos(phase).astype(np.float32), np.sin(phase).astype(np.float32)


def plane_tables(side):
    column = np.arange(G * HZ)
    cell = np.arange(side)[:, None]
    phase_y = (cell * (column // HZ)[None, :] % G) * (2.0 * math.pi / G)
    phase_z = (cell * (column % HZ)[None, :] % G) * (2.0 * math.pi / G)
    cy = jnp.asarray(np.cos(phase_y).astype(np.float32))[:, None, :]
    sy = jnp.asarray(np.sin(phase_y).astype(np.float32))[:, None, :]
    cz = jnp.asarray(np.cos(phase_z).astype(np.float32))[None, :, :]
    sz = jnp.asarray(np.sin(phase_z).astype(np.float32))[None, :, :]
    cos_t = (cy * cz - sy * sz).reshape(side * side, G * HZ)
    sin_t = (sy * cz + cy * sz).reshape(side * side, G * HZ)
    return cos_t, sin_t


def split_bf16(table):
    upper = table.astype(jnp.bfloat16)
    lower = (table - upper.astype(jnp.float32)).astype(jnp.bfloat16)
    return upper, lower


def mix_table(cell_count):
    cos_x, sin_x = line_table(G, cell_count)
    return jnp.asarray(np.concatenate([cos_x, sin_x], axis=0))


def dot2(rows, upper, lower):
    first = jnp.dot(rows, upper, preferred_element_type=jnp.float32)
    second = jnp.dot(rows, lower, preferred_element_type=jnp.float32)
    return first + second


def receptor_spectra(grids, cos_hi, cos_lo, sin_hi, sin_lo):
    terms, rows, cells = grids.shape
    receptors = rows // G
    flat = grids.reshape(terms * rows, cells)
    plane_re = dot2(flat, cos_hi, cos_lo).reshape(terms, receptors, G, G * HZ)
    plane_ims = dot2(flat, sin_hi, sin_lo).reshape(terms, receptors, G, G * HZ)
    mix = mix_table(G)
    mixed_re = jnp.einsum("px,trxq->trpq", mix, plane_re, precision=HIGH)
    mixed_ims = jnp.einsum("px,trxq->trpq", mix, plane_ims, precision=HIGH)
    spec_re = mixed_re[:, :, :G] - mixed_ims[:, :, G:]
    spec_im = -mixed_ims[:, :, :G] - mixed_re[:, :, G:]
    return spec_re, spec_im


def ligand_spectra(voxels, coefficients, box_cos, box_sin):
    rot_count = voxels.shape[1]
    terms = coefficients.shape[0]
    flat_index = (voxels[0] * LB + voxels[1]) * LB + voxels[2]
    cells = jnp.arange(LB**3, dtype=jnp.int32)
    onehot = (flat_index[:, :, None] == cells[None, None, :]).astype(jnp.float32)
    grid = jnp.einsum("ta,nac->tnc", coefficients, onehot, precision=HIGHEST)
    grid = grid.reshape(terms, rot_count, LB, LB * LB)
    plane_re = jnp.einsum("tnxc,cq->tnxq", grid, box_cos, precision=HIGH)
    plane_ims = jnp.einsum("tnxc,cq->tnxq", grid, box_sin, precision=HIGH)
    mix = mix_table(LB)
    mixed_re = jnp.einsum("px,tnxq->tnpq", mix, plane_re, precision=HIGH)
    mixed_ims = jnp.einsum("px,tnxq->tnpq", mix, plane_ims, precision=HIGH)
    lig_re = mixed_re[:, :, :G] - mixed_ims[:, :, G:]
    lig_im = -mixed_ims[:, :, :G] - mixed_re[:, :, G:]
    return lig_re, lig_im


def correlate(lig_re, lig_im, rec_re, rec_im):
    lr = lig_re[:, None]
    li = lig_im[:, None]
    rr = rec_re[:, :, None]
    ri = rec_im[:, :, None]
    prod_re = jnp.sum(lr * rr + li * ri, axis=0)
    prod_im = jnp.sum(lr * ri - li * rr, axis=0)
    return jnp.stack([prod_re, prod_im], axis=0)


def inverse_scores(products, cos_t, sin_t):
    mix = mix_table(G)
    mixed = jnp.einsum("xp,srnpq->srnxq", mix, products, precision=HIGH)
    inv_re = mixed[0, :, :, :G] - mixed[1, :, :, G:]
    inv_im = mixed[1, :, :, :G] + mixed[0, :, :, G:]
    freq_z = np.arange(G * HZ) % HZ
    fold = np.where((freq_z == 0) | (freq_z == G // 2), 1.0, 2.0) / float(G**3)
    fold = jnp.asarray(fold.astype(np.float32))
    scores = jnp.einsum("rnxq,cq->rnxc", inv_re * fold, cos_t, precision=HIGH)
    scores = scores - jnp.einsum("rnxq,cq->rnxc", inv_im * fold, sin_t, precision=HIGH)
    return scores


def reduce_scatter_terms(products, term_count):
    share = products.shape[2] // term_count
    here = lax.axis_index("term")
    total = lax.dynamic_slice_in_dim(products, here * share, share, axis=2)
    for shift in range(1, term_count):
        target = (here + shift) % term_count
        outgoing = lax.dynamic_slice_in_dim(products, target * share, share, axis=2)
        pairs = [(k, (k + shift) % term_count) for k in range(term_count)]
        total = total + lax.ppermute(outgoing, "term", pairs)
    return total


def make_body(term_count):
    def body(receptor_grids, term_weights, atom_weights, ligand_cells):
        gathered = lax.all_gather(receptor_grids, "rot", axis=1, tiled=True)
        with jax.named_scope("twiddle_tables"):
            cos_t, sin_t = plane_tables(G)
            box_cos, box_sin = plane_tables(LB)
            cos_hi, cos_lo = split_bf16(cos_t)
            sin_hi, sin_lo = split_bf16(sin_t)
            tables = lax.optimization_barrier(
                (cos_t, sin_t, box_cos, box_sin, cos_hi, cos_lo, sin_hi, sin_lo)
            )
            cos_t, sin_t, box_cos, box_sin, cos_hi, cos_lo, sin_hi, sin_lo = tables
        with jax.named_scope("ligand_spectra"):
            coefficients = atom_weights * term_weights[:, None]
            lig_re, lig_im = ligand_spectra(ligand_cells, coefficients, box_cos, box_sin)
        with jax.named_scope("receptor_spectra"):
            rec_re, rec_im = receptor_spectra(gathered, cos_hi, cos_lo, sin_hi, sin_lo)
        with jax.named_scope("correlate"):
            products = correlate(lig_re, lig_im, rec_re, rec_im)
        products = reduce_scatter_terms(products, term_count)
        with jax.named_scope("inverse_scores"):
            scores = inverse_scores(products, cos_t, sin_t)
            best_here = jnp.max(scores, axis=(2, 3))
        best_scores = lax.all_gather(best_here, "term", axis=1, tiled=True)
        best_all = lax.all_gather(best_scores, "rot", axis=1, tiled=True)
        best_overall = jnp.max(best_all, axis=1)
        return (best_scores, best_overall)

    return body


def solution(mesh):
    placed = (P("term", "rot", None), P("term"), P("term", None), P(None, "rot", None))
    return jax.shard_map(
        make_body(mesh.shape["term"]),
        mesh=mesh,
        in_specs=placed,
        out_specs=(P(None, "rot"), P()),
        check_vma=False,
    )
```

```python
import math

import numpy as np

import jax
import jax.numpy as jnp
from jax import lax
from jax.sharding import PartitionSpec as P

G = 32
HZ = G // 2 + 1
LB = 16

HIGH = lax.Precision.HIGH
HIGHEST = lax.Precision.HIGHEST


def line_table(freq_count, cell_count):
    freq = np.arange(freq_count)[:, None]
    cell = np.arange(cell_count)[None, :]
    phase = (freq * cell % G).astype(np.float64) * (2.0 * math.pi / G)
    return np.cos(phase).astype(np.float32), np.sin(phase).astype(np.float32)


def plane_tables(side):
    column = np.arange(G * HZ)
    cell = np.arange(side)[:, None]
    phase_y = (cell * (column // HZ)[None, :] % G) * (2.0 * math.pi / G)
    phase_z = (cell * (column % HZ)[None, :] % G) * (2.0 * math.pi / G)
    cy = jnp.asarray(np.cos(phase_y).astype(np.float32))[:, None, :]
    sy = jnp.asarray(np.sin(phase_y).astype(np.float32))[:, None, :]
    cz = jnp.asarray(np.cos(phase_z).astype(np.float32))[None, :, :]
    sz = jnp.asarray(np.sin(phase_z).astype(np.float32))[None, :, :]
    cos_t = cy * cz - sy * sz
    sin_t = sy * cz + cy * sz
    return jnp.concatenate([cos_t, sin_t], axis=-1).reshape(side * side, 2 * G * HZ)


def split_bf16(table):
    upper = table.astype(jnp.bfloat16)
    lower = (table - upper.astype(jnp.float32)).astype(jnp.bfloat16)
    return upper, lower


def mix_table(cell_count):
    cos_x, sin_x = line_table(G, cell_count)
    return jnp.asarray(np.concatenate([cos_x, sin_x], axis=0))


def receptor_mixed(grids, table_hi, table_lo):
    terms, rows, cells = grids.shape
    receptors = rows // G
    flat = grids.reshape(terms * rows, cells)
    plane = jnp.dot(flat, table_hi, preferred_element_type=jnp.float32)
    plane = plane + jnp.dot(flat, table_lo, preferred_element_type=jnp.float32)
    plane = plane.reshape(terms, receptors, G, 2 * G * HZ)
    return jnp.einsum("px,trxq->trpq", mix_table(G), plane, precision=HIGH)


def ligand_coefficients(voxels, coefficients, box_table):
    rot_count = voxels.shape[1]
    terms = coefficients.shape[0]
    width = G * HZ
    flat_index = (voxels[0] * LB + voxels[1]) * LB + voxels[2]
    cells = jnp.arange(LB**3, dtype=jnp.int32)
    onehot = (flat_index[:, :, None] == cells[None, None, :]).astype(jnp.float32)
    grid = jnp.einsum("ta,nac->tnc", coefficients, onehot, precision=HIGHEST)
    grid = grid.reshape(terms, rot_count, LB, LB * LB)
    plane = jnp.einsum("tnxc,cq->tnxq", grid, box_table, precision=HIGH)
    mixed = jnp.einsum("px,tnxq->tnpq", mix_table(LB), plane, precision=HIGH)
    lig_re = mixed[:, :, :G, :width] - mixed[:, :, G:, width:]
    lig_im = -mixed[:, :, :G, width:] - mixed[:, :, G:, :width]
    first = jnp.concatenate([lig_re, -lig_im], axis=-1)
    second = jnp.concatenate([-lig_im, -lig_re], axis=-1)
    third = jnp.concatenate([-lig_re, lig_im], axis=-1)
    return first, second, third


def correlate(mixed, first, second, third):
    rec_cos = mixed[:, :, None, :G]
    rec_sin = mixed[:, :, None, G:]
    a = first[:, None]
    b = second[:, None]
    d = third[:, None]
    part_re = jnp.sum(rec_cos * a + rec_sin * b, axis=0)
    part_im = jnp.sum(rec_cos * b + rec_sin * d, axis=0)
    return part_re, part_im


def inverse_scores(products, full_table):
    width = G * HZ
    mixed = jnp.einsum("xp,srnpq->srnxq", mix_table(G), products, precision=HIGH)
    inv_re = mixed[0, :, :, :G] - mixed[1, :, :, G:]
    inv_im = mixed[1, :, :, :G] + mixed[0, :, :, G:]
    freq_z = np.arange(width) % HZ
    fold = np.where((freq_z == 0) | (freq_z == G // 2), 1.0, 2.0) / float(G**3)
    fold = jnp.asarray(fold.astype(np.float32))
    joined = jnp.concatenate([inv_re * fold, -inv_im * fold], axis=-1)
    return jnp.einsum("rnxq,cq->rnxc", joined, full_table, precision=HIGH)


def reduce_scatter_terms(products, term_count):
    share = products.shape[2] // term_count
    here = lax.axis_index("term")
    total = lax.dynamic_slice_in_dim(products, here * share, share, axis=2)
    for shift in range(1, term_count):
        target = (here + shift) % term_count
        outgoing = lax.dynamic_slice_in_dim(products, target * share, share, axis=2)
        pairs = [(k, (k + shift) % term_count) for k in range(term_count)]
        total = total + lax.ppermute(outgoing, "term", pairs)
    return total


def max_over_rot(values, rot_count):
    if rot_count & (rot_count - 1):
        gathered = lax.all_gather(values, "rot", axis=0, tiled=True)
        return jnp.max(gathered, axis=0, keepdims=True)
    shift = 1
    while shift < rot_count:
        pairs = [(k, k ^ shift) for k in range(rot_count)]
        values = jnp.maximum(values, lax.ppermute(values, "rot", pairs))
        shift *= 2
    return values


def make_body(term_count, rot_count):
    def body(receptor_grids, term_weights, atom_weights, ligand_cells):
        terms_here = receptor_grids.shape[0]
        cut = (terms_here + 1) // 2
        chunks = [(0, cut), (cut, terms_here)]
        gathered = [
            lax.all_gather(receptor_grids[lo:hi], "rot", axis=1, tiled=True) for lo, hi in chunks
        ]
        with jax.named_scope("twiddle_tables"):
            full_table = plane_tables(G)
            box_table = plane_tables(LB)
            table_hi, table_lo = split_bf16(full_table)
            tables = lax.optimization_barrier((full_table, box_table, table_hi, table_lo))
            full_table, box_table, table_hi, table_lo = tables
        with jax.named_scope("ligand_spectra"):
            coefficients = atom_weights * term_weights[:, None]
            first, second, third = ligand_coefficients(ligand_cells, coefficients, box_table)
        part_re = 0.0
        part_im = 0.0
        for (lo, hi), grids in zip(chunks, gathered):
            with jax.named_scope("receptor_spectra"):
                mixed = receptor_mixed(grids, table_hi, table_lo)
            with jax.named_scope("correlate"):
                add_re, add_im = correlate(mixed, first[lo:hi], second[lo:hi], third[lo:hi])
            part_re = part_re + add_re
            part_im = part_im + add_im
        width = G * HZ
        prod_re = part_re[..., :width] + part_re[..., width:]
        prod_im = part_im[..., :width] + part_im[..., width:]
        products = jnp.stack([prod_re, prod_im], axis=0)
        products = reduce_scatter_terms(products, term_count)
        with jax.named_scope("inverse_scores"):
            scores = inverse_scores(products, full_table)
            best_here = jnp.max(scores, axis=(2, 3))
        best_scores = lax.all_gather(best_here, "term", axis=1, tiled=True)
        best_overall = max_over_rot(jnp.max(best_scores, axis=1)[None], rot_count)[0]
        return (best_scores, best_overall)

    return body


def solution(mesh):
    placed = (P("term", "rot", None), P("term"), P("term", None), P(None, "rot", None))
    return jax.shard_map(
        make_body(mesh.shape["term"], mesh.shape["rot"]),
        mesh=mesh,
        in_specs=placed,
        out_specs=(P(None, "rot"), P()),
        check_vma=False,
    )
```

```python
import math

import numpy as np

import jax
import jax.numpy as jnp
from jax import lax
from jax.sharding import PartitionSpec as P

G = 32
HZ = G // 2 + 1
LB = 16

HIGH = lax.Precision.HIGH
HIGHEST = lax.Precision.HIGHEST


def line_table(freq_count, cell_count):
    freq = np.arange(freq_count)[:, None]
    cell = np.arange(cell_count)[None, :]
    phase = (freq * cell % G).astype(np.float64) * (2.0 * math.pi / G)
    return np.cos(phase).astype(np.float32), np.sin(phase).astype(np.float32)


def plane_tables(side):
    column = np.arange(G * HZ)
    cell = np.arange(side)[:, None]
    phase_y = (cell * (column // HZ)[None, :] % G) * (2.0 * math.pi / G)
    phase_z = (cell * (column % HZ)[None, :] % G) * (2.0 * math.pi / G)
    cy = jnp.asarray(np.cos(phase_y).astype(np.float32))[:, None, :]
    sy = jnp.asarray(np.sin(phase_y).astype(np.float32))[:, None, :]
    cz = jnp.asarray(np.cos(phase_z).astype(np.float32))[None, :, :]
    sz = jnp.asarray(np.sin(phase_z).astype(np.float32))[None, :, :]
    cos_t = cy * cz - sy * sz
    sin_t = sy * cz + cy * sz
    return jnp.concatenate([cos_t, sin_t], axis=-1).reshape(side * side, 2 * G * HZ)


def split_bf16(table):
    upper = table.astype(jnp.bfloat16)
    lower = (table - upper.astype(jnp.float32)).astype(jnp.bfloat16)
    return upper, lower


def mix_table(cell_count):
    cos_x, sin_x = line_table(G, cell_count)
    return jnp.asarray(np.concatenate([cos_x, sin_x], axis=0))


def receptor_mixed(grids, table_hi, table_lo):
    terms, rows, cells = grids.shape
    receptors = rows // G
    flat = grids.reshape(terms * rows, cells)
    plane = jnp.dot(flat, table_hi, preferred_element_type=jnp.float32)
    plane = plane + jnp.dot(flat, table_lo, preferred_element_type=jnp.float32)
    plane = plane.reshape(terms, receptors, G, 2 * G * HZ)
    return jnp.einsum("px,trxq->trpq", mix_table(G), plane, precision=HIGH)


def ligand_coefficients(voxels, coefficients, box_table):
    rot_count = voxels.shape[1]
    terms = coefficients.shape[0]
    width = G * HZ
    flat_index = (voxels[0] * LB + voxels[1]) * LB + voxels[2]
    cells = jnp.arange(LB**3, dtype=jnp.int32)
    onehot = (flat_index[:, :, None] == cells[None, None, :]).astype(jnp.float32)
    grid = jnp.einsum("ta,nac->tnc", coefficients, onehot, precision=HIGHEST)
    grid = grid.reshape(terms, rot_count, LB, LB * LB)
    plane = jnp.einsum("tnxc,cq->tnxq", grid, box_table, precision=HIGH)
    mixed = jnp.einsum("px,tnxq->tnpq", mix_table(LB), plane, precision=HIGH)
    lig_re = mixed[:, :, :G, :width] - mixed[:, :, G:, width:]
    lig_im = -mixed[:, :, :G, width:] - mixed[:, :, G:, :width]
    first = jnp.concatenate([lig_re, -lig_im], axis=-1)
    second = jnp.concatenate([-lig_im, -lig_re], axis=-1)
    third = jnp.concatenate([-lig_re, lig_im], axis=-1)
    return first, second, third


def correlate(mixed, first, second, third):
    rec_cos = mixed[:, :, None, :G]
    rec_sin = mixed[:, :, None, G:]
    a = first[:, None]
    b = second[:, None]
    d = third[:, None]
    part_re = jnp.sum(rec_cos * a + rec_sin * b, axis=0)
    part_im = jnp.sum(rec_cos * b + rec_sin * d, axis=0)
    return part_re, part_im


def inverse_scores(products, full_table):
    width = G * HZ
    mixed = jnp.einsum("xp,srnpq->srnxq", mix_table(G), products, precision=HIGH)
    inv_re = mixed[0, :, :, :G] - mixed[1, :, :, G:]
    inv_im = mixed[1, :, :, :G] + mixed[0, :, :, G:]
    freq_z = np.arange(width) % HZ
    fold = np.where((freq_z == 0) | (freq_z == G // 2), 1.0, 2.0) / float(G**3)
    fold = jnp.asarray(fold.astype(np.float32))
    joined = jnp.concatenate([inv_re * fold, -inv_im * fold], axis=-1)
    return jnp.einsum("rnxq,cq->rnxc", joined, full_table, precision=HIGH)


def butterfly_max(values, axes, device_count):
    shift = 1
    while shift < device_count:
        pairs = [(k, k ^ shift) for k in range(device_count)]
        values = jnp.maximum(values, lax.ppermute(values, axes, pairs))
        shift *= 2
    return values


def make_body(plane_count, inner_count, term_count):
    all_axes = ("plane", "inner", "term")

    def body(receptor_grids, term_weights, atom_weights, ligand_cells):
        terms_here, rows_here, cells = receptor_grids.shape
        rot_here = ligand_cells.shape[1]
        rot_total = rot_here * plane_count * inner_count
        plane = lax.axis_index("plane")
        inner = lax.axis_index("inner")
        term = lax.axis_index("term")
        gathered = lax.all_gather(receptor_grids, ("term", "inner"), axis=0, tiled=False)
        gathered = gathered.reshape(term_count, inner_count, terms_here, rows_here, cells)
        gathered = jnp.transpose(gathered, (0, 2, 1, 3, 4))
        gathered = gathered.reshape(term_count * terms_here, inner_count * rows_here, cells)
        cells_here = lax.all_gather(ligand_cells, "plane", axis=1, tiled=True)
        share = cells_here.shape[1] // term_count
        voxels = lax.dynamic_slice_in_dim(cells_here, term * share, share, axis=1)
        local = term * share + jnp.arange(share, dtype=jnp.int32)
        rot_ids = ((local // rot_here) * inner_count + inner) * rot_here + local % rot_here
        coefficients = atom_weights * term_weights[:, None]
        coefficients = lax.all_gather(coefficients, "term", axis=0, tiled=True)
        with jax.named_scope("twiddle_tables"):
            full_table = plane_tables(G)
            box_table = plane_tables(LB)
            table_hi, table_lo = split_bf16(full_table)
            tables = lax.optimization_barrier((full_table, box_table, table_hi, table_lo))
            full_table, box_table, table_hi, table_lo = tables
        with jax.named_scope("ligand_spectra"):
            first, second, third = ligand_coefficients(voxels, coefficients, box_table)
        with jax.named_scope("receptor_spectra"):
            mixed = receptor_mixed(gathered, table_hi, table_lo)
        with jax.named_scope("correlate"):
            part_re, part_im = correlate(mixed, first, second, third)
        width = G * HZ
        prod_re = part_re[..., :width] + part_re[..., width:]
        prod_im = part_im[..., :width] + part_im[..., width:]
        products = jnp.stack([prod_re, prod_im], axis=0)
        with jax.named_scope("inverse_scores"):
            scores = inverse_scores(products, full_table)
            best_here = jnp.max(scores, axis=(2, 3))[0]
        receptors = plane_count
        columns = jnp.arange(rot_total, dtype=jnp.int32)
        hit = rot_ids[:, None] == columns[None, :]
        row = jnp.max(jnp.where(hit, best_here[:, None], -jnp.inf), axis=0)
        mine = jnp.arange(receptors, dtype=jnp.int32)[:, None] == plane
        placed = jnp.where(mine, row[None, :], -jnp.inf)
        placed = butterfly_max(placed, all_axes, plane_count * inner_count * term_count)
        start = (plane * inner_count + inner) * rot_here
        best_scores = lax.dynamic_slice_in_dim(placed, start, rot_here, axis=1)
        best_overall = jnp.max(placed, axis=1)
        return (best_scores, best_overall)

    return body


def solution(mesh):
    rot_count = mesh.shape["rot"]
    term_count = mesh.shape["term"]

    def run(receptor_grids, term_weights, atom_weights, ligand_cells):
        receptors = receptor_grids.shape[1] // G
        inner_count = rot_count // receptors
        devices = np.asarray(mesh.devices).reshape(receptors, inner_count, term_count)
        fine = jax.sharding.Mesh(devices, ("plane", "inner", "term"))
        rows = ("plane", "inner")
        placed = (P("term", rows, None), P("term"), P("term", None), P(None, rows, None))
        mapped = jax.shard_map(
            make_body(receptors, inner_count, term_count),
            mesh=fine,
            in_specs=placed,
            out_specs=(P(None, rows), P()),
            check_vma=False,
        )
        return mapped(receptor_grids, term_weights, atom_weights, ligand_cells)

    return run
```

```python
import math

import numpy as np

import jax
import jax.numpy as jnp
from jax import lax
from jax.sharding import PartitionSpec as P

G = 32
HZ = G // 2 + 1
LB = 16
WIDTH = 640

HIGH = lax.Precision.HIGH
HIGHEST = lax.Precision.HIGHEST


def line_table(freq_count, cell_count):
    freq = np.arange(freq_count)[:, None]
    cell = np.arange(cell_count)[None, :]
    phase = (freq * cell % G).astype(np.float64) * (2.0 * math.pi / G)
    return np.cos(phase).astype(np.float32), np.sin(phase).astype(np.float32)


def plane_tables(side):
    column = np.arange(G * HZ)
    cell = np.arange(side)[:, None]
    phase_y = (cell * (column // HZ)[None, :] % G) * (2.0 * math.pi / G)
    phase_z = (cell * (column % HZ)[None, :] % G) * (2.0 * math.pi / G)
    cy = jnp.asarray(np.cos(phase_y).astype(np.float32))[:, None, :]
    sy = jnp.asarray(np.sin(phase_y).astype(np.float32))[:, None, :]
    cz = jnp.asarray(np.cos(phase_z).astype(np.float32))[None, :, :]
    sz = jnp.asarray(np.sin(phase_z).astype(np.float32))[None, :, :]
    cos_t = cy * cz - sy * sz
    sin_t = sy * cz + cy * sz
    pad = jnp.zeros((side, side, WIDTH - G * HZ), jnp.float32)
    joined = jnp.concatenate([cos_t, pad, sin_t, pad], axis=-1)
    return joined.reshape(side * side, 2 * WIDTH)


def split_bf16(table):
    upper = table.astype(jnp.bfloat16)
    lower = (table - upper.astype(jnp.float32)).astype(jnp.bfloat16)
    return upper, lower


def mix_table(cell_count):
    cos_x, sin_x = line_table(G, cell_count)
    return jnp.asarray(np.concatenate([cos_x, sin_x], axis=0))


def receptor_mixed(grids, table_hi, table_lo):
    terms, rows, cells = grids.shape
    receptors = rows // G
    flat = grids.reshape(terms * rows, cells)
    plane = jnp.dot(flat, table_hi, preferred_element_type=jnp.float32)
    plane = plane + jnp.dot(flat, table_lo, preferred_element_type=jnp.float32)
    plane = plane.reshape(terms, receptors, G, 2 * WIDTH)
    return jnp.einsum("px,trxq->trpq", mix_table(G), plane, precision=HIGH)


def ligand_spectra(voxels, coefficients, box_table):
    yz_index = voxels[1] * LB + voxels[2]
    rows = jnp.take(box_table, yz_index, axis=0)
    x_cells = jnp.arange(LB, dtype=jnp.int32)
    in_x = (voxels[0][:, None, :] == x_cells[None, :, None]).astype(jnp.float32)
    weights = coefficients[None, :, None, :] * in_x[:, None, :, :]
    plane = jnp.einsum("ntxa,naq->tnxq", weights, rows, precision=HIGH)
    mixed = jnp.einsum("px,tnxq->tnpq", mix_table(LB), plane, precision=HIGH)
    lig_re = mixed[:, :, :G, :WIDTH] - mixed[:, :, G:, WIDTH:]
    lig_im = -mixed[:, :, :G, WIDTH:] - mixed[:, :, G:, :WIDTH]
    return lig_re, lig_im


def correlate(mixed, lig_re, lig_im):
    re_cos = mixed[:, :, None, :G, :WIDTH]
    re_sin = mixed[:, :, None, G:, :WIDTH]
    ims_cos = mixed[:, :, None, :G, WIDTH:]
    ims_sin = mixed[:, :, None, G:, WIDTH:]
    lr = lig_re[:, None]
    li = lig_im[:, None]
    prod_re = jnp.sum(re_cos * lr - re_sin * li - ims_sin * lr - ims_cos * li, axis=0)
    prod_im = jnp.sum(-ims_cos * lr - re_sin * lr - re_cos * li + ims_sin * li, axis=0)
    return jnp.stack([prod_re, prod_im], axis=0)


def inverse_scores(products, full_table):
    mixed = jnp.einsum("xp,srnpq->srnxq", mix_table(G), products, precision=HIGH)
    inv_re = mixed[0, :, :, :G] - mixed[1, :, :, G:]
    inv_im = mixed[1, :, :, :G] + mixed[0, :, :, G:]
    column = np.arange(WIDTH)
    freq_z = column % HZ
    fold = np.where((freq_z == 0) | (freq_z == G // 2), 1.0, 2.0) / float(G**3)
    fold = np.where(column < G * HZ, fold, 0.0)
    fold = jnp.asarray(fold.astype(np.float32))
    joined = jnp.concatenate([inv_re * fold, -inv_im * fold], axis=-1)
    return jnp.einsum("rnxq,cq->rnxc", joined, full_table, precision=HIGH)


def gather_by_permutes(values, axis_name, count, here):
    blocks = [values]
    for shift in range(1, count):
        pairs = [(k, (k + shift) % count) for k in range(count)]
        blocks.append(lax.ppermute(values, axis_name, pairs))
    return blocks


def butterfly_max(values, axes, device_count):
    shift = 1
    while shift < device_count:
        pairs = [(k, k ^ shift) for k in range(device_count)]
        values = jnp.maximum(values, lax.ppermute(values, axes, pairs))
        shift *= 2
    return values


def make_body(plane_count, inner_count, term_count):
    all_axes = ("plane", "inner", "term")

    def body(receptor_grids, term_weights, atom_weights, ligand_cells):
        terms_here, rows_here, cells = receptor_grids.shape
        rot_here = ligand_cells.shape[1]
        rot_total = rot_here * plane_count * inner_count
        plane = lax.axis_index("plane")
        inner = lax.axis_index("inner")
        term = lax.axis_index("term")
        gathered = lax.all_gather(receptor_grids, ("term", "inner"), axis=0, tiled=False)
        gathered = gathered.reshape(term_count, inner_count, terms_here, rows_here, cells)
        gathered = jnp.transpose(gathered, (0, 2, 1, 3, 4))
        gathered = gathered.reshape(term_count * terms_here, inner_count * rows_here, cells)
        cell_blocks = gather_by_permutes(ligand_cells, "plane", plane_count, plane)
        cells_here = jnp.concatenate(cell_blocks, axis=1)
        share = cells_here.shape[1] // term_count
        voxels = lax.dynamic_slice_in_dim(cells_here, term * share, share, axis=1)
        local = term * share + jnp.arange(share, dtype=jnp.int32)
        source_plane = (plane - local // rot_here) % plane_count
        rot_ids = (source_plane * inner_count + inner) * rot_here + local % rot_here
        coefficients = atom_weights * term_weights[:, None]
        term_blocks = jnp.stack(gather_by_permutes(coefficients, "term", term_count, term))
        order = (term - jnp.arange(term_count, dtype=jnp.int32)) % term_count
        coefficients = jnp.take(term_blocks, order, axis=0).reshape(-1, coefficients.shape[1])
        with jax.named_scope("twiddle_tables"):
            full_table = plane_tables(G)
            box_table = plane_tables(LB)
            table_hi, table_lo = split_bf16(full_table)
            tables = lax.optimization_barrier((full_table, box_table, table_hi, table_lo))
            full_table, box_table, table_hi, table_lo = tables
        with jax.named_scope("ligand_spectra"):
            lig_re, lig_im = ligand_spectra(voxels, coefficients, box_table)
        with jax.named_scope("receptor_spectra"):
            mixed = receptor_mixed(gathered, table_hi, table_lo)
        with jax.named_scope("correlate"):
            products = correlate(mixed, lig_re, lig_im)
        with jax.named_scope("inverse_scores"):
            scores = inverse_scores(products, full_table)
            best_here = jnp.max(scores, axis=(2, 3))[0]
        receptors = plane_count
        columns = jnp.arange(rot_total, dtype=jnp.int32)
        hit = rot_ids[:, None] == columns[None, :]
        row = jnp.max(jnp.where(hit, best_here[:, None], -jnp.inf), axis=0)
        mine = jnp.arange(receptors, dtype=jnp.int32)[:, None] == plane
        placed = jnp.where(mine, row[None, :], -jnp.inf)
        placed = butterfly_max(placed, all_axes, plane_count * inner_count * term_count)
        start = (plane * inner_count + inner) * rot_here
        best_scores = lax.dynamic_slice_in_dim(placed, start, rot_here, axis=1)
        best_overall = jnp.max(placed, axis=1)
        return (best_scores, best_overall)

    return body


def solution(mesh):
    rot_count = mesh.shape["rot"]
    term_count = mesh.shape["term"]

    def run(receptor_grids, term_weights, atom_weights, ligand_cells):
        receptors = receptor_grids.shape[1] // G
        inner_count = rot_count // receptors
        devices = np.asarray(mesh.devices).reshape(receptors, inner_count, term_count)
        fine = jax.sharding.Mesh(devices, ("plane", "inner", "term"))
        rows = ("plane", "inner")
        placed = (P("term", rows, None), P("term"), P("term", None), P(None, rows, None))
        mapped = jax.shard_map(
            make_body(receptors, inner_count, term_count),
            mesh=fine,
            in_specs=placed,
            out_specs=(P(None, rows), P()),
            check_vma=False,
        )
        return mapped(receptor_grids, term_weights, atom_weights, ligand_cells)

    return run
```

```python
import math

import numpy as np

import jax
import jax.numpy as jnp
from jax import lax
from jax.sharding import PartitionSpec as P

G = 32
HZ = G // 2 + 1
LB = 16
WIDTH = 640

HIGH = lax.Precision.HIGH
HIGHEST = lax.Precision.HIGHEST


def line_table(freq_count, cell_count):
    freq = np.arange(freq_count)[:, None]
    cell = np.arange(cell_count)[None, :]
    phase = (freq * cell % G).astype(np.float64) * (2.0 * math.pi / G)
    return np.cos(phase).astype(np.float32), np.sin(phase).astype(np.float32)


def plane_factors():
    column = np.arange(2 * WIDTH)
    half = column // WIDTH
    freq = column % WIDTH
    valid = freq < G * HZ
    cell = np.arange(G)[:, None]
    phase_y = (cell * (freq // HZ)[None, :] % G) * (2.0 * math.pi / G)
    phase_z = (cell * (freq % HZ)[None, :] % G) * (2.0 * math.pi / G)
    cy, sy = np.cos(phase_y), np.sin(phase_y)
    cz, sz = np.cos(phase_z), np.sin(phase_z)
    first = np.where(half == 0, cy, sy) * valid
    third = np.where(half == 0, -sy, cy) * valid
    return [jnp.asarray(f.astype(np.float32)) for f in (first, cz, third, sz)]


def plane_table(factors, side):
    first, second, third, fourth = [f[:side] for f in factors]
    table = first[:, None, :] * second[None, :, :] + third[:, None, :] * fourth[None, :, :]
    return table.reshape(side * side, 2 * WIDTH)


def split_bf16(table):
    upper = lax.reduce_precision(table, exponent_bits=8, mantissa_bits=7)
    lower = table - upper
    return upper.astype(jnp.bfloat16), lower.astype(jnp.bfloat16)


def mix_tables(cell_count):
    cos_x, sin_x = line_table(G, cell_count)
    from_cos = np.concatenate([cos_x, -sin_x], axis=0)
    from_sin = np.concatenate([-sin_x, -cos_x], axis=0)
    return jnp.asarray(from_cos), jnp.asarray(from_sin)


def mix_table(cell_count):
    cos_x, sin_x = line_table(G, cell_count)
    return jnp.asarray(np.concatenate([cos_x, sin_x], axis=0))


def x_transform(plane, cell_count, form):
    from_cos, from_sin = mix_tables(cell_count)
    first = jnp.einsum(form, from_cos, plane[..., :WIDTH], precision=HIGH)
    return first + jnp.einsum(form, from_sin, plane[..., WIDTH:], precision=HIGH)


def receptor_mixed(grids, table_hi, table_lo):
    terms, rows, cells = grids.shape
    receptors = rows // G
    flat = grids.reshape(terms * rows, cells)
    plane = jnp.dot(flat, table_hi, preferred_element_type=jnp.float32)
    plane = plane + jnp.dot(flat, table_lo, preferred_element_type=jnp.float32)
    plane = plane.reshape(terms, receptors, G, 2 * WIDTH)
    return x_transform(plane, G, "px,trxq->trpq")


def ligand_spectra(voxels, coefficients, box_table):
    yz_index = voxels[1] * LB + voxels[2]
    rows = jnp.take(box_table, yz_index, axis=0)
    x_cells = jnp.arange(LB, dtype=jnp.int32)
    in_x = (voxels[0][:, None, :] == x_cells[None, :, None]).astype(jnp.float32)
    weights = coefficients[None, :, None, :] * in_x[:, None, :, :]
    plane = jnp.einsum("ntxa,naq->tnxq", weights, rows, precision=HIGH)
    return x_transform(plane, LB, "px,tnxq->tnpq")


def correlate(rec_spec, lig_spec):
    rr = rec_spec[:, :, None, :G]
    ri = rec_spec[:, :, None, G:]
    lr = lig_spec[:, None, :, :G]
    li = lig_spec[:, None, :, G:]
    prod_re = jnp.sum(lr * rr + li * ri, axis=0)
    prod_im = jnp.sum(lr * ri - li * rr, axis=0)
    return jnp.stack([prod_re, prod_im], axis=0)


def inverse_scores(products, table_hi, table_lo):
    mixed = jnp.einsum("xp,srnpq->srnxq", mix_table(G), products, precision=HIGH)
    inv_re = mixed[0, :, :, :G] - mixed[1, :, :, G:]
    inv_im = mixed[1, :, :, :G] + mixed[0, :, :, G:]
    column = np.arange(WIDTH)
    freq_z = column % HZ
    fold = np.where((freq_z == 0) | (freq_z == G // 2), 1.0, 2.0) / float(G**3)
    fold = np.where(column < G * HZ, fold, 0.0)
    fold = jnp.asarray(fold.astype(np.float32))
    joined = jnp.concatenate([inv_re * fold, -inv_im * fold], axis=-1)
    upper, lower = lax.optimization_barrier(split_bf16(joined))
    form = "rnxq,cq->rnxc"
    scores = jnp.einsum(form, upper, table_hi, preferred_element_type=jnp.float32)
    scores = scores + jnp.einsum(form, lower, table_hi, preferred_element_type=jnp.float32)
    return scores + jnp.einsum(form, upper, table_lo, preferred_element_type=jnp.float32)


def gather_by_permutes(values, axis_name, count, here):
    blocks = [values]
    for shift in range(1, count):
        pairs = [(k, (k + shift) % count) for k in range(count)]
        blocks.append(lax.ppermute(values, axis_name, pairs))
    return blocks


def butterfly_max(values, axes, device_count):
    stride = 1
    while stride < device_count:
        radix = 4 if stride * 4 <= device_count else 2
        received = []
        for digit in range(1, radix):
            pairs = [(k, k ^ (digit * stride)) for k in range(device_count)]
            received.append(lax.ppermute(values, axes, pairs))
        for block in received:
            values = jnp.maximum(values, block)
        stride *= radix
    return values


def make_body(plane_count, inner_count, term_count):
    all_axes = ("plane", "inner", "term")

    def body(receptor_grids, term_weights, atom_weights, ligand_cells):
        terms_here, rows_here, cells = receptor_grids.shape
        rot_here = ligand_cells.shape[1]
        rot_total = rot_here * plane_count * inner_count
        plane = lax.axis_index("plane")
        inner = lax.axis_index("inner")
        term = lax.axis_index("term")
        gathered = lax.all_gather(receptor_grids, ("term", "inner"), axis=0, tiled=False)
        gathered = gathered.reshape(term_count, inner_count, terms_here, rows_here, cells)
        gathered = jnp.transpose(gathered, (0, 2, 1, 3, 4))
        gathered = gathered.reshape(term_count * terms_here, inner_count * rows_here, cells)
        cell_blocks = gather_by_permutes(ligand_cells, "plane", plane_count, plane)
        cells_here = jnp.concatenate(cell_blocks, axis=1)
        share = cells_here.shape[1] // term_count
        voxels = lax.dynamic_slice_in_dim(cells_here, term * share, share, axis=1)
        local = term * share + jnp.arange(share, dtype=jnp.int32)
        source_plane = (plane - local // rot_here) % plane_count
        rot_ids = (source_plane * inner_count + inner) * rot_here + local % rot_here
        coefficients = atom_weights * term_weights[:, None]
        term_blocks = jnp.stack(gather_by_permutes(coefficients, "term", term_count, term))
        order = (term - jnp.arange(term_count, dtype=jnp.int32)) % term_count
        coefficients = jnp.take(term_blocks, order, axis=0).reshape(-1, coefficients.shape[1])
        with jax.named_scope("twiddle_tables"):
            factors = plane_factors()
            table_hi, table_lo = split_bf16(plane_table(factors, G))
            box_table = plane_table(factors, LB)
            tables = lax.optimization_barrier((box_table, table_hi, table_lo))
            box_table, table_hi, table_lo = tables
        with jax.named_scope("ligand_spectra"):
            lig_spec = ligand_spectra(voxels, coefficients, box_table)
        with jax.named_scope("receptor_spectra"):
            rec_spec = receptor_mixed(gathered, table_hi, table_lo)
        with jax.named_scope("correlate"):
            products = correlate(rec_spec, lig_spec)
        with jax.named_scope("inverse_scores"):
            scores = inverse_scores(products, table_hi, table_lo)
            best_here = jnp.max(scores, axis=(2, 3))[0]
        receptors = plane_count
        columns = jnp.arange(rot_total, dtype=jnp.int32)
        hit = rot_ids[:, None] == columns[None, :]
        row = jnp.max(jnp.where(hit, best_here[:, None], -jnp.inf), axis=0)
        mine = jnp.arange(receptors, dtype=jnp.int32)[:, None] == plane
        placed = jnp.where(mine, row[None, :], -jnp.inf)
        placed = butterfly_max(placed, all_axes, plane_count * inner_count * term_count)
        start = (plane * inner_count + inner) * rot_here
        best_scores = lax.dynamic_slice_in_dim(placed, start, rot_here, axis=1)
        best_overall = jnp.max(placed, axis=1)
        return (best_scores, best_overall)

    return body


def solution(mesh):
    rot_count = mesh.shape["rot"]
    term_count = mesh.shape["term"]

    def run(receptor_grids, term_weights, atom_weights, ligand_cells):
        receptors = receptor_grids.shape[1] // G
        inner_count = rot_count // receptors
        devices = np.asarray(mesh.devices).reshape(receptors, inner_count, term_count)
        fine = jax.sharding.Mesh(devices, ("plane", "inner", "term"))
        rows = ("plane", "inner")
        placed = (P("term", rows, None), P("term"), P("term", None), P(None, rows, None))
        mapped = jax.shard_map(
            make_body(receptors, inner_count, term_count),
            mesh=fine,
            in_specs=placed,
            out_specs=(P(None, rows), P()),
            check_vma=False,
        )
        return mapped(receptor_grids, term_weights, atom_weights, ligand_cells)

    return run
```

```python
import math

import numpy as np

import jax
import jax.numpy as jnp
from jax import lax
from jax.sharding import PartitionSpec as P

G = 32
HZ = G // 2 + 1
LB = 16
WIDTH = 640

HIGH = lax.Precision.HIGH
HIGHEST = lax.Precision.HIGHEST


def line_table(freq_count, cell_count):
    freq = np.arange(freq_count)[:, None]
    cell = np.arange(cell_count)[None, :]
    phase = (freq * cell % G).astype(np.float64) * (2.0 * math.pi / G)
    return np.cos(phase).astype(np.float32), np.sin(phase).astype(np.float32)


def plane_factors():
    column = np.arange(2 * WIDTH)
    half = column // WIDTH
    freq = column % WIDTH
    valid = freq < G * HZ
    cell = np.arange(G)[:, None]
    phase_y = (cell * (freq // HZ)[None, :] % G) * (2.0 * math.pi / G)
    phase_z = (cell * (freq % HZ)[None, :] % G) * (2.0 * math.pi / G)
    cy, sy = np.cos(phase_y), np.sin(phase_y)
    cz, sz = np.cos(phase_z), np.sin(phase_z)
    first = np.where(half == 0, cy, sy) * valid
    third = np.where(half == 0, -sy, cy) * valid
    return [jnp.asarray(f.astype(np.float32)) for f in (first, cz, third, sz)]


def plane_table(factors, side):
    first, second, third, fourth = [
        jnp.transpose(f[:side].reshape(side, 2, WIDTH), (1, 0, 2)) for f in factors
    ]
    table = first[:, :, None, :] * second[:, None, :, :] + third[:, :, None, :] * fourth[:, None, :, :]
    return table.reshape(2, side * side, WIDTH)


def split_bf16(table):
    upper = lax.reduce_precision(table, exponent_bits=8, mantissa_bits=7)
    lower = table - upper
    return upper.astype(jnp.bfloat16), lower.astype(jnp.bfloat16)


def mix_tables(cell_count):
    cos_x, sin_x = line_table(G, cell_count)
    from_cos = np.concatenate([cos_x, -sin_x], axis=0)
    from_sin = np.concatenate([-sin_x, -cos_x], axis=0)
    return jnp.asarray(np.concatenate([from_cos, from_sin], axis=1))


def mix_table(cell_count):
    cos_x, sin_x = line_table(G, cell_count)
    return jnp.asarray(np.concatenate([cos_x, sin_x], axis=0))


def receptor_mixed(grids, table_hi, table_lo):
    terms, rows, cells = grids.shape
    receptors = rows // G
    grids = grids.reshape(terms, receptors, G, cells)
    form = "trxc,hcq->trhxq"
    plane = jnp.einsum(form, grids, table_hi, preferred_element_type=jnp.float32)
    plane = plane + jnp.einsum(form, grids, table_lo, preferred_element_type=jnp.float32)
    plane = plane.reshape(terms, receptors, 2 * G, WIDTH)
    return jnp.einsum("pk,trkq->trpq", mix_tables(G), plane, precision=HIGH)


def ligand_spectra(voxels, coefficients, box_table):
    yz_index = voxels[1] * LB + voxels[2]
    cells = jnp.arange(LB * LB, dtype=jnp.int32)
    onehot = (yz_index[:, :, None] == cells[None, None, :]).astype(jnp.bfloat16)
    x_cells = jnp.arange(LB, dtype=jnp.int32)
    in_x = (voxels[0][:, None, :] == x_cells[None, :, None]).astype(jnp.float32)
    weights = coefficients[None, :, None, :] * in_x[:, None, :, :]
    upper, lower = split_bf16(weights)
    form = "ntxa,nac->ntxc"
    grid = jnp.einsum(form, upper, onehot, preferred_element_type=jnp.float32)
    grid = grid + jnp.einsum(form, lower, onehot, preferred_element_type=jnp.float32)
    plane = jnp.einsum("ntxc,hcq->nthxq", grid, box_table, precision=HIGH)
    rot_count, terms = plane.shape[0], plane.shape[1]
    plane = plane.reshape(rot_count, terms, 2 * LB, WIDTH)
    return jnp.einsum("pk,ntkq->tnpq", mix_tables(LB), plane, precision=HIGH)


def correlate(rec_spec, lig_spec):
    rr = rec_spec[:, :, None, :G]
    ri = rec_spec[:, :, None, G:]
    lr = lig_spec[:, None, :, :G]
    li = lig_spec[:, None, :, G:]
    prod_re = jnp.sum(lr * rr + li * ri, axis=0)
    prod_im = jnp.sum(lr * ri - li * rr, axis=0)
    return jnp.stack([prod_re, prod_im], axis=0)


def inverse_scores(products, table_hi, table_lo):
    mixed = jnp.einsum("xp,srnpq->srnxq", mix_table(G), products, precision=HIGH)
    inv_re = mixed[0, :, :, :G] - mixed[1, :, :, G:]
    inv_im = mixed[1, :, :, :G] + mixed[0, :, :, G:]
    column = np.arange(WIDTH)
    freq_z = column % HZ
    fold = np.where((freq_z == 0) | (freq_z == G // 2), 1.0, 2.0) / float(G**3)
    fold = np.where(column < G * HZ, fold, 0.0)
    fold = jnp.asarray(fold.astype(np.float32))
    joined = jnp.stack([inv_re * fold, -inv_im * fold], axis=3)
    upper, lower = lax.optimization_barrier(split_bf16(joined))
    form = "rnxhq,hcq->rnxc"
    scores = jnp.einsum(form, upper, table_hi, preferred_element_type=jnp.float32)
    scores = scores + jnp.einsum(form, lower, table_hi, preferred_element_type=jnp.float32)
    return scores + jnp.einsum(form, upper, table_lo, preferred_element_type=jnp.float32)


def gather_by_permutes(values, axis_name, count, here):
    blocks = [values]
    for shift in range(1, count):
        pairs = [(k, (k + shift) % count) for k in range(count)]
        blocks.append(lax.ppermute(values, axis_name, pairs))
    return blocks


def butterfly_max(values, axes, device_count):
    stride = 1
    while stride < device_count:
        radix = 4 if stride * 4 <= device_count else 2
        received = []
        for digit in range(1, radix):
            pairs = [(k, k ^ (digit * stride)) for k in range(device_count)]
            received.append(lax.ppermute(values, axes, pairs))
        for block in received:
            values = jnp.maximum(values, block)
        stride *= radix
    return values


def make_body(plane_count, inner_count, term_count):
    all_axes = ("plane", "inner", "term")

    def body(receptor_grids, term_weights, atom_weights, ligand_cells):
        terms_here, rows_here, cells = receptor_grids.shape
        rot_here = ligand_cells.shape[1]
        rot_total = rot_here * plane_count * inner_count
        plane = lax.axis_index("plane")
        inner = lax.axis_index("inner")
        term = lax.axis_index("term")
        gathered = lax.all_gather(receptor_grids, ("term", "inner"), axis=0, tiled=False)
        gathered = gathered.reshape(term_count, inner_count, terms_here, rows_here, cells)
        gathered = jnp.transpose(gathered, (0, 2, 1, 3, 4))
        gathered = gathered.reshape(term_count * terms_here, inner_count * rows_here, cells)
        cell_blocks = gather_by_permutes(ligand_cells, "plane", plane_count, plane)
        cells_here = jnp.concatenate(cell_blocks, axis=1)
        share = cells_here.shape[1] // term_count
        voxels = lax.dynamic_slice_in_dim(cells_here, term * share, share, axis=1)
        local = term * share + jnp.arange(share, dtype=jnp.int32)
        source_plane = (plane - local // rot_here) % plane_count
        rot_ids = (source_plane * inner_count + inner) * rot_here + local % rot_here
        coefficients = atom_weights * term_weights[:, None]
        term_blocks = jnp.stack(gather_by_permutes(coefficients, "term", term_count, term))
        order = (term - jnp.arange(term_count, dtype=jnp.int32)) % term_count
        coefficients = jnp.take(term_blocks, order, axis=0).reshape(-1, coefficients.shape[1])
        with jax.named_scope("twiddle_tables"):
            factors = plane_factors()
            table_hi, table_lo = split_bf16(plane_table(factors, G))
            box_table = plane_table(factors, LB)
            tables = lax.optimization_barrier((box_table, table_hi, table_lo))
            box_table, table_hi, table_lo = tables
        with jax.named_scope("ligand_spectra"):
            lig_spec = ligand_spectra(voxels, coefficients, box_table)
        with jax.named_scope("receptor_spectra"):
            rec_spec = receptor_mixed(gathered, table_hi, table_lo)
        with jax.named_scope("correlate"):
            products = correlate(rec_spec, lig_spec)
        with jax.named_scope("inverse_scores"):
            scores = inverse_scores(products, table_hi, table_lo)
            best_here = jnp.max(scores, axis=(2, 3))[0]
        receptors = plane_count
        columns = jnp.arange(rot_total, dtype=jnp.int32)
        hit = rot_ids[:, None] == columns[None, :]
        row = jnp.max(jnp.where(hit, best_here[:, None], -jnp.inf), axis=0)
        mine = jnp.arange(receptors, dtype=jnp.int32)[:, None] == plane
        placed = jnp.where(mine, row[None, :], -jnp.inf)
        placed = butterfly_max(placed, all_axes, plane_count * inner_count * term_count)
        start = (plane * inner_count + inner) * rot_here
        best_scores = lax.dynamic_slice_in_dim(placed, start, rot_here, axis=1)
        best_overall = jnp.max(placed, axis=1)
        return (best_scores, best_overall)

    return body


def solution(mesh):
    rot_count = mesh.shape["rot"]
    term_count = mesh.shape["term"]

    def run(receptor_grids, term_weights, atom_weights, ligand_cells):
        receptors = receptor_grids.shape[1] // G
        inner_count = rot_count // receptors
        devices = np.asarray(mesh.devices).reshape(receptors, inner_count, term_count)
        fine = jax.sharding.Mesh(devices, ("plane", "inner", "term"))
        rows = ("plane", "inner")
        placed = (P("term", rows, None), P("term"), P("term", None), P(None, rows, None))
        mapped = jax.shard_map(
            make_body(receptors, inner_count, term_count),
            mesh=fine,
            in_specs=placed,
            out_specs=(P(None, rows), P()),
            check_vma=False,
        )
        return mapped(receptor_grids, term_weights, atom_weights, ligand_cells)

    return run
```

```python
import math

import numpy as np

import jax
import jax.numpy as jnp
from jax import lax
from jax.sharding import PartitionSpec as P

G = 32
HZ = G // 2 + 1
LB = 16
WIDTH = 640

HIGH = lax.Precision.HIGH
HIGHEST = lax.Precision.HIGHEST


def line_table(freq_count, cell_count):
    freq = np.arange(freq_count)[:, None]
    cell = np.arange(cell_count)[None, :]
    phase = (freq * cell % G).astype(np.float64) * (2.0 * math.pi / G)
    return np.cos(phase).astype(np.float32), np.sin(phase).astype(np.float32)


def plane_factors():
    column = np.arange(2 * WIDTH)
    half = column // WIDTH
    freq = column % WIDTH
    valid = freq < G * HZ
    cell = np.arange(G)[:, None]
    phase_y = (cell * (freq // HZ)[None, :] % G) * (2.0 * math.pi / G)
    phase_z = (cell * (freq % HZ)[None, :] % G) * (2.0 * math.pi / G)
    cy, sy = np.cos(phase_y), np.sin(phase_y)
    cz, sz = np.cos(phase_z), np.sin(phase_z)
    first = np.where(half == 0, cy, sy) * valid
    third = np.where(half == 0, -sy, cy) * valid
    return [jnp.asarray(f.astype(np.float32)) for f in (first, cz, third, sz)]


def plane_table(factors, side):
    first, second, third, fourth = [
        jnp.transpose(f[:side].reshape(side, 2, WIDTH), (1, 0, 2)) for f in factors
    ]
    table = first[:, :, None, :] * second[:, None, :, :] + third[:, :, None, :] * fourth[:, None, :, :]
    return table.reshape(2, side * side, WIDTH)


def split_bf16(table):
    upper = lax.reduce_precision(table, exponent_bits=8, mantissa_bits=7)
    lower = table - upper
    return upper.astype(jnp.bfloat16), lower.astype(jnp.bfloat16)


def mix_tables(cell_count):
    cos_x, sin_x = line_table(G, cell_count)
    from_cos = np.concatenate([cos_x, -sin_x], axis=0)
    from_sin = np.concatenate([-sin_x, -cos_x], axis=0)
    return jnp.asarray(np.concatenate([from_cos, from_sin], axis=1))


def mix_table(cell_count):
    cos_x, sin_x = line_table(G, cell_count)
    return jnp.asarray(np.concatenate([cos_x, sin_x], axis=0))


def receptor_mixed(grids, table_hi, table_lo):
    terms, rows, cells = grids.shape
    receptors = rows // G
    grids = grids.reshape(terms, receptors, G, cells)
    form = "trxc,hcq->trhxq"
    plane = jnp.einsum(form, grids, table_hi, preferred_element_type=jnp.float32)
    plane = plane + jnp.einsum(form, grids, table_lo, preferred_element_type=jnp.float32)
    plane = plane.reshape(terms, receptors, 2 * G, WIDTH)
    return jnp.einsum("pk,trkq->trpq", mix_tables(G), plane, precision=HIGH)


def ligand_spectra(voxels, coefficients, box_table):
    yz_index = voxels[1] * LB + voxels[2]
    cells = jnp.arange(LB * LB, dtype=jnp.int32)
    onehot = (yz_index[:, :, None] == cells[None, None, :]).astype(jnp.bfloat16)
    x_cells = jnp.arange(LB, dtype=jnp.int32)
    in_x = (voxels[0][:, None, :] == x_cells[None, :, None]).astype(jnp.float32)
    weights = coefficients[None, :, None, :] * in_x[:, None, :, :]
    upper, lower = split_bf16(weights)
    form = "ntxa,nac->ntxc"
    grid = jnp.einsum(form, upper, onehot, preferred_element_type=jnp.float32)
    grid = grid + jnp.einsum(form, lower, onehot, preferred_element_type=jnp.float32)
    plane = jnp.einsum("ntxc,hcq->nthxq", grid, box_table, precision=HIGH)
    rot_count, terms = plane.shape[0], plane.shape[1]
    plane = plane.reshape(rot_count, terms, 2 * LB, WIDTH)
    return jnp.einsum("pk,ntkq->tnpq", mix_tables(LB), plane, precision=HIGH)


def correlate(rec_spec, lig_spec):
    rr = rec_spec[:, :, None, :G]
    ri = rec_spec[:, :, None, G:]
    lr = lig_spec[:, None, :, :G]
    li = lig_spec[:, None, :, G:]
    prod_re = jnp.sum(lr * rr + li * ri, axis=0)
    prod_im = jnp.sum(lr * ri - li * rr, axis=0)
    return jnp.stack([prod_re, prod_im], axis=0)


def inverse_scores(products, table_hi, table_lo):
    mixed = jnp.einsum("xp,srnpq->srnxq", mix_table(G), products, precision=HIGH)
    inv_re = mixed[0, :, :, :G] - mixed[1, :, :, G:]
    inv_im = mixed[1, :, :, :G] + mixed[0, :, :, G:]
    column = np.arange(WIDTH)
    freq_z = column % HZ
    fold = np.where((freq_z == 0) | (freq_z == G // 2), 1.0, 2.0) / float(G**3)
    fold = np.where(column < G * HZ, fold, 0.0)
    fold = jnp.asarray(fold.astype(np.float32))
    joined = jnp.stack([inv_re * fold, -inv_im * fold], axis=3)
    upper, lower = lax.optimization_barrier(split_bf16(joined))
    form = "rnxhq,hcq->rnxc"
    scores = jnp.einsum(form, upper, table_hi, preferred_element_type=jnp.float32)
    scores = scores + jnp.einsum(form, lower, table_hi, preferred_element_type=jnp.float32)
    return scores + jnp.einsum(form, upper, table_lo, preferred_element_type=jnp.float32)


def gather_by_permutes(values, axis_name, count, here):
    blocks = [values]
    for shift in range(1, count):
        pairs = [(k, (k + shift) % count) for k in range(count)]
        blocks.append(lax.ppermute(values, axis_name, pairs))
    return blocks


def butterfly_max(values, axes, device_count):
    stride = 1
    while stride < device_count:
        radix = 4 if stride * 4 <= device_count else 2
        received = []
        for digit in range(1, radix):
            pairs = [(k, k ^ (digit * stride)) for k in range(device_count)]
            received.append(lax.ppermute(values, axes, pairs))
        for block in received:
            values = jnp.maximum(values, block)
        stride *= radix
    return values


def make_body(plane_count, inner_count, term_count):
    all_axes = ("plane", "inner", "term")

    def body(receptor_grids, term_weights, atom_weights, ligand_cells):
        terms_here, rows_here, cells = receptor_grids.shape
        rot_here = ligand_cells.shape[1]
        rot_total = rot_here * plane_count * inner_count
        plane = lax.axis_index("plane")
        inner = lax.axis_index("inner")
        term = lax.axis_index("term")
        group = inner_count * term_count
        if group <= 8:
            here = inner * term_count + term
            blocks = jnp.stack(gather_by_permutes(receptor_grids, ("inner", "term"), group, here))
            order = (here - jnp.arange(group, dtype=jnp.int32)) % group
            gathered = jnp.take(blocks, order, axis=0)
            gathered = gathered.reshape(inner_count, term_count, terms_here, rows_here, cells)
            gathered = jnp.transpose(gathered, (1, 2, 0, 3, 4))
        else:
            gathered = lax.all_gather(receptor_grids, ("term", "inner"), axis=0, tiled=False)
            gathered = gathered.reshape(term_count, inner_count, terms_here, rows_here, cells)
            gathered = jnp.transpose(gathered, (0, 2, 1, 3, 4))
        gathered = gathered.reshape(term_count * terms_here, inner_count * rows_here, cells)
        cell_blocks = gather_by_permutes(ligand_cells, "plane", plane_count, plane)
        cells_here = jnp.concatenate(cell_blocks, axis=1)
        share = cells_here.shape[1] // term_count
        voxels = lax.dynamic_slice_in_dim(cells_here, term * share, share, axis=1)
        local = term * share + jnp.arange(share, dtype=jnp.int32)
        source_plane = (plane - local // rot_here) % plane_count
        rot_ids = (source_plane * inner_count + inner) * rot_here + local % rot_here
        coefficients = atom_weights * term_weights[:, None]
        term_blocks = jnp.stack(gather_by_permutes(coefficients, "term", term_count, term))
        order = (term - jnp.arange(term_count, dtype=jnp.int32)) % term_count
        coefficients = jnp.take(term_blocks, order, axis=0).reshape(-1, coefficients.shape[1])
        with jax.named_scope("twiddle_tables"):
            factors = plane_factors()
            table_hi, table_lo = split_bf16(plane_table(factors, G))
            box_table = plane_table(factors, LB)
            tables = lax.optimization_barrier((box_table, table_hi, table_lo))
            box_table, table_hi, table_lo = tables
        with jax.named_scope("ligand_spectra"):
            lig_spec = ligand_spectra(voxels, coefficients, box_table)
        with jax.named_scope("receptor_spectra"):
            rec_spec = receptor_mixed(gathered, table_hi, table_lo)
        with jax.named_scope("correlate"):
            products = correlate(rec_spec, lig_spec)
        with jax.named_scope("inverse_scores"):
            scores = inverse_scores(products, table_hi, table_lo)
            best_here = jnp.max(scores, axis=(2, 3))[0]
        receptors = plane_count
        columns = jnp.arange(rot_total, dtype=jnp.int32)
        hit = rot_ids[:, None] == columns[None, :]
        row = jnp.max(jnp.where(hit, best_here[:, None], -jnp.inf), axis=0)
        mine = jnp.arange(receptors, dtype=jnp.int32)[:, None] == plane
        placed = jnp.where(mine, row[None, :], -jnp.inf)
        placed = butterfly_max(placed, all_axes, plane_count * inner_count * term_count)
        start = (plane * inner_count + inner) * rot_here
        best_scores = lax.dynamic_slice_in_dim(placed, start, rot_here, axis=1)
        best_overall = jnp.max(placed, axis=1)
        return (best_scores, best_overall)

    return body


def solution(mesh):
    rot_count = mesh.shape["rot"]
    term_count = mesh.shape["term"]

    def run(receptor_grids, term_weights, atom_weights, ligand_cells):
        receptors = receptor_grids.shape[1] // G
        inner_count = rot_count // receptors
        devices = np.asarray(mesh.devices).reshape(receptors, inner_count, term_count)
        fine = jax.sharding.Mesh(devices, ("plane", "inner", "term"))
        rows = ("plane", "inner")
        placed = (P("term", rows, None), P("term"), P("term", None), P(None, rows, None))
        mapped = jax.shard_map(
            make_body(receptors, inner_count, term_count),
            mesh=fine,
            in_specs=placed,
            out_specs=(P(None, rows), P()),
            check_vma=False,
        )
        return mapped(receptor_grids, term_weights, atom_weights, ligand_cells)

    return run
```

```python
import math

import numpy as np

import jax
import jax.numpy as jnp
from jax import lax
from jax.sharding import PartitionSpec as P

G = 32
HZ = G // 2 + 1
LB = 16
WIDTH = 640

HIGH = lax.Precision.HIGH
HIGHEST = lax.Precision.HIGHEST


def line_table(freq_count, cell_count):
    freq = np.arange(freq_count)[:, None]
    cell = np.arange(cell_count)[None, :]
    phase = (freq * cell % G).astype(np.float64) * (2.0 * math.pi / G)
    return np.cos(phase).astype(np.float32), np.sin(phase).astype(np.float32)


def plane_factors():
    column = np.arange(2 * WIDTH)
    half = column // WIDTH
    freq = column % WIDTH
    valid = freq < G * HZ
    cell = np.arange(G)[:, None]
    phase_y = (cell * (freq // HZ)[None, :] % G) * (2.0 * math.pi / G)
    phase_z = (cell * (freq % HZ)[None, :] % G) * (2.0 * math.pi / G)
    cy, sy = np.cos(phase_y), np.sin(phase_y)
    cz, sz = np.cos(phase_z), np.sin(phase_z)
    first = np.where(half == 0, cy, sy) * valid
    third = np.where(half == 0, -sy, cy) * valid
    return [jnp.asarray(f.astype(np.float32)) for f in (first, cz, third, sz)]


def plane_table(factors, side):
    first, second, third, fourth = [
        jnp.transpose(f[:side].reshape(side, 2, WIDTH), (1, 0, 2)) for f in factors
    ]
    table = first[:, :, None, :] * second[:, None, :, :] + third[:, :, None, :] * fourth[:, None, :, :]
    return table.reshape(2, side * side, WIDTH)


def split_bf16(table):
    upper = lax.reduce_precision(table, exponent_bits=8, mantissa_bits=7)
    lower = table - upper
    return upper.astype(jnp.bfloat16), lower.astype(jnp.bfloat16)


def mix_tables(cell_count):
    cos_x, sin_x = line_table(G, cell_count)
    from_cos = np.concatenate([cos_x, -sin_x], axis=0)
    from_sin = np.concatenate([-sin_x, -cos_x], axis=0)
    return jnp.asarray(np.concatenate([from_cos, from_sin], axis=1))


def mix_table(cell_count):
    cos_x, sin_x = line_table(G, cell_count)
    return jnp.asarray(np.concatenate([cos_x, sin_x], axis=0))


def receptor_mixed(grids, table_hi, table_lo):
    terms, rows, cells = grids.shape
    receptors = rows // G
    grids = grids.reshape(terms, receptors, G, cells)
    form = "trxc,hcq->trhxq"
    plane = jnp.einsum(form, grids, table_hi, preferred_element_type=jnp.float32)
    plane = plane + jnp.einsum(form, grids, table_lo, preferred_element_type=jnp.float32)
    plane = plane.reshape(terms, receptors, 2 * G, WIDTH)
    return jnp.einsum("pk,trkq->trpq", mix_tables(G), plane, precision=HIGH)


def ligand_spectra(voxels, coefficients, box_table):
    yz_index = voxels[1] * LB + voxels[2]
    cells = jnp.arange(LB * LB, dtype=jnp.int32)
    onehot = (yz_index[:, :, None] == cells[None, None, :]).astype(jnp.bfloat16)
    x_cells = jnp.arange(LB, dtype=jnp.int32)
    in_x = (voxels[0][:, None, :] == x_cells[None, :, None]).astype(jnp.float32)
    weights = coefficients[None, :, None, :] * in_x[:, None, :, :]
    upper, lower = split_bf16(weights)
    form = "ntxa,nac->ntxc"
    grid = jnp.einsum(form, upper, onehot, preferred_element_type=jnp.float32)
    grid = grid + jnp.einsum(form, lower, onehot, preferred_element_type=jnp.float32)
    plane = jnp.einsum("ntxc,hcq->nthxq", grid, box_table, precision=HIGH)
    rot_count, terms = plane.shape[0], plane.shape[1]
    plane = plane.reshape(rot_count, terms, 2 * LB, WIDTH)
    return jnp.einsum("pk,ntkq->tnpq", mix_tables(LB), plane, precision=HIGH)


def correlate(rec_spec, lig_spec):
    rr = rec_spec[:, :, None, :G]
    ri = rec_spec[:, :, None, G:]
    lr = lig_spec[:, None, :, :G]
    li = lig_spec[:, None, :, G:]
    prod_re = jnp.sum(lr * rr + li * ri, axis=0)
    prod_im = jnp.sum(lr * ri - li * rr, axis=0)
    return jnp.stack([prod_re, prod_im], axis=0)


def inverse_scores(products, table_hi, table_lo):
    mixed = jnp.einsum("xp,srnpq->srnxq", mix_table(G), products, precision=HIGH)
    inv_re = mixed[0, :, :, :G] - mixed[1, :, :, G:]
    inv_im = mixed[1, :, :, :G] + mixed[0, :, :, G:]
    column = np.arange(WIDTH)
    freq_z = column % HZ
    fold = np.where((freq_z == 0) | (freq_z == G // 2), 1.0, 2.0) / float(G**3)
    fold = np.where(column < G * HZ, fold, 0.0)
    fold = jnp.asarray(fold.astype(np.float32))
    joined = jnp.stack([inv_re * fold, -inv_im * fold], axis=3)
    upper, lower = lax.optimization_barrier(split_bf16(joined))
    form = "rnxhq,hcq->rnxc"
    scores = jnp.einsum(form, upper, table_hi, preferred_element_type=jnp.float32)
    scores = scores + jnp.einsum(form, lower, table_hi, preferred_element_type=jnp.float32)
    return scores + jnp.einsum(form, upper, table_lo, preferred_element_type=jnp.float32)


def gather_by_permutes(values, axis_name, count, here):
    blocks = [values]
    for shift in range(1, count):
        pairs = [(k, (k + shift) % count) for k in range(count)]
        blocks.append(lax.ppermute(values, axis_name, pairs))
    return blocks


def butterfly_max(values, axes, device_count):
    stride = 1
    while stride < device_count:
        radix = 4 if stride * 4 <= device_count else 2
        received = []
        for digit in range(1, radix):
            pairs = [(k, k ^ (digit * stride)) for k in range(device_count)]
            received.append(lax.ppermute(values, axes, pairs))
        for block in received:
            values = jnp.maximum(values, block)
        stride *= radix
    return values


def make_body(plane_count, inner_count, term_count):
    all_axes = ("plane", "inner", "term")

    def body(receptor_grids, term_weights, atom_weights, ligand_cells):
        terms_here, rows_here, cells = receptor_grids.shape
        rot_here = ligand_cells.shape[1]
        rot_total = rot_here * plane_count * inner_count
        plane = lax.axis_index("plane")
        inner = lax.axis_index("inner")
        term = lax.axis_index("term")
        groups = [lax.all_gather(receptor_grids, "inner", axis=1, tiled=True)]
        for shift in range(1, term_count):
            pairs = [(k, (k + shift) % term_count) for k in range(term_count)]
            moved = lax.ppermute(receptor_grids, "term", pairs)
            groups.append(lax.all_gather(moved, "inner", axis=1, tiled=True))
        cell_blocks = gather_by_permutes(ligand_cells, "plane", plane_count, plane)
        cells_here = jnp.concatenate(cell_blocks, axis=1)
        share = cells_here.shape[1] // term_count
        voxels = lax.dynamic_slice_in_dim(cells_here, term * share, share, axis=1)
        local = term * share + jnp.arange(share, dtype=jnp.int32)
        source_plane = (plane - local // rot_here) % plane_count
        rot_ids = (source_plane * inner_count + inner) * rot_here + local % rot_here
        coefficients = atom_weights * term_weights[:, None]
        coefficients = jnp.concatenate(gather_by_permutes(coefficients, "term", term_count, term))
        with jax.named_scope("twiddle_tables"):
            factors = plane_factors()
            table_hi, table_lo = split_bf16(plane_table(factors, G))
            box_table = plane_table(factors, LB)
            tables = lax.optimization_barrier((box_table, table_hi, table_lo))
            box_table, table_hi, table_lo = tables
        with jax.named_scope("ligand_spectra"):
            lig_spec = ligand_spectra(voxels, coefficients, box_table)
        products = 0.0
        for index, grids in enumerate(groups):
            lo = index * terms_here
            with jax.named_scope("receptor_spectra"):
                rec_spec = receptor_mixed(grids, table_hi, table_lo)
            with jax.named_scope("correlate"):
                products = products + correlate(rec_spec, lig_spec[lo : lo + terms_here])
        with jax.named_scope("inverse_scores"):
            scores = inverse_scores(products, table_hi, table_lo)
            best_here = jnp.max(scores, axis=(2, 3))[0]
        receptors = plane_count
        columns = jnp.arange(rot_total, dtype=jnp.int32)
        hit = rot_ids[:, None] == columns[None, :]
        row = jnp.max(jnp.where(hit, best_here[:, None], -jnp.inf), axis=0)
        mine = jnp.arange(receptors, dtype=jnp.int32)[:, None] == plane
        placed = jnp.where(mine, row[None, :], -jnp.inf)
        placed = butterfly_max(placed, all_axes, plane_count * inner_count * term_count)
        start = (plane * inner_count + inner) * rot_here
        best_scores = lax.dynamic_slice_in_dim(placed, start, rot_here, axis=1)
        best_overall = jnp.max(placed, axis=1)
        return (best_scores, best_overall)

    return body


def solution(mesh):
    rot_count = mesh.shape["rot"]
    term_count = mesh.shape["term"]

    def run(receptor_grids, term_weights, atom_weights, ligand_cells):
        receptors = receptor_grids.shape[1] // G
        inner_count = rot_count // receptors
        devices = np.asarray(mesh.devices).reshape(receptors, inner_count, term_count)
        fine = jax.sharding.Mesh(devices, ("plane", "inner", "term"))
        rows = ("plane", "inner")
        placed = (P("term", rows, None), P("term"), P("term", None), P(None, rows, None))
        mapped = jax.shard_map(
            make_body(receptors, inner_count, term_count),
            mesh=fine,
            in_specs=placed,
            out_specs=(P(None, rows), P()),
            check_vma=False,
        )
        return mapped(receptor_grids, term_weights, atom_weights, ligand_cells)

    return run
```

```python
import math

import numpy as np

import jax
import jax.numpy as jnp
from jax import lax
from jax.sharding import PartitionSpec as P

G = 32
HZ = G // 2 + 1
LB = 16
WIDTH = 640

HIGH = lax.Precision.HIGH
HIGHEST = lax.Precision.HIGHEST


def line_table(freq_count, cell_count):
    freq = np.arange(freq_count)[:, None]
    cell = np.arange(cell_count)[None, :]
    phase = (freq * cell % G).astype(np.float64) * (2.0 * math.pi / G)
    return np.cos(phase).astype(np.float32), np.sin(phase).astype(np.float32)


def plane_factors():
    column = np.arange(2 * WIDTH)
    half = column // WIDTH
    freq = column % WIDTH
    valid = freq < G * HZ
    cell = np.arange(G)[:, None]
    phase_y = (cell * (freq // HZ)[None, :] % G) * (2.0 * math.pi / G)
    phase_z = (cell * (freq % HZ)[None, :] % G) * (2.0 * math.pi / G)
    cy, sy = np.cos(phase_y), np.sin(phase_y)
    cz, sz = np.cos(phase_z), np.sin(phase_z)
    first = np.where(half == 0, cy, sy) * valid
    third = np.where(half == 0, -sy, cy) * valid
    return [jnp.asarray(f.astype(np.float32)) for f in (first, cz, third, sz)]


def plane_table(factors, side):
    first, second, third, fourth = [
        jnp.transpose(f[:side].reshape(side, 2, WIDTH), (1, 0, 2)) for f in factors
    ]
    table = first[:, :, None, :] * second[:, None, :, :] + third[:, :, None, :] * fourth[:, None, :, :]
    return table.reshape(2, side * side, WIDTH)


def split_bf16(table):
    upper = lax.reduce_precision(table, exponent_bits=8, mantissa_bits=7)
    lower = table - upper
    return upper.astype(jnp.bfloat16), lower.astype(jnp.bfloat16)


def mix_tables(cell_count):
    cos_x, sin_x = line_table(G, cell_count)
    from_cos = np.concatenate([cos_x, -sin_x], axis=0)
    from_sin = np.concatenate([-sin_x, -cos_x], axis=0)
    return jnp.asarray(np.concatenate([from_cos, from_sin], axis=1))


def mix_table(cell_count):
    cos_x, sin_x = line_table(G, cell_count)
    return jnp.asarray(np.concatenate([cos_x, sin_x], axis=0))


def receptor_mixed(grids, table_hi, table_lo):
    terms, rows, cells = grids.shape
    receptors = rows // G
    grids = grids.reshape(terms, receptors, G, cells)
    form = "trxc,hcq->trhxq"
    plane = jnp.einsum(form, grids, table_hi, preferred_element_type=jnp.float32)
    plane = plane + jnp.einsum(form, grids, table_lo, preferred_element_type=jnp.float32)
    plane = plane.reshape(terms, receptors, 2 * G, WIDTH)
    return jnp.einsum("pk,trkq->trpq", mix_tables(G), plane, precision=HIGH)


def ligand_spectra(voxels, coefficients, box_table):
    yz_index = voxels[1] * LB + voxels[2]
    cells = jnp.arange(LB * LB, dtype=jnp.int32)
    onehot = (yz_index[:, :, None] == cells[None, None, :]).astype(jnp.bfloat16)
    x_cells = jnp.arange(LB, dtype=jnp.int32)
    in_x = (voxels[0][:, None, :] == x_cells[None, :, None]).astype(jnp.float32)
    weights = coefficients[None, :, None, :] * in_x[:, None, :, :]
    upper, lower = split_bf16(weights)
    form = "ntxa,nac->ntxc"
    grid = jnp.einsum(form, upper, onehot, preferred_element_type=jnp.float32)
    grid = grid + jnp.einsum(form, lower, onehot, preferred_element_type=jnp.float32)
    plane = jnp.einsum("ntxc,hcq->nthxq", grid, box_table, precision=HIGH)
    rot_count, terms = plane.shape[0], plane.shape[1]
    plane = plane.reshape(rot_count, terms, 2 * LB, WIDTH)
    return jnp.einsum("pk,ntkq->tnpq", mix_tables(LB), plane, precision=HIGH)


def correlate(rec_spec, lig_spec):
    rr = rec_spec[:, :, None, :G]
    ri = rec_spec[:, :, None, G:]
    lr = lig_spec[:, None, :, :G]
    li = lig_spec[:, None, :, G:]
    prod_re = jnp.sum(lr * rr + li * ri, axis=0)
    prod_im = jnp.sum(lr * ri - li * rr, axis=0)
    return jnp.stack([prod_re, prod_im], axis=0)


def inverse_scores(products, table_hi, table_lo):
    mixed = jnp.einsum("xp,srnpq->srnxq", mix_table(G), products, precision=HIGH)
    inv_re = mixed[0, :, :, :G] - mixed[1, :, :, G:]
    inv_im = mixed[1, :, :, :G] + mixed[0, :, :, G:]
    column = np.arange(WIDTH)
    freq_z = column % HZ
    fold = np.where((freq_z == 0) | (freq_z == G // 2), 1.0, 2.0) / float(G**3)
    fold = np.where(column < G * HZ, fold, 0.0)
    fold = jnp.asarray(fold.astype(np.float32))
    joined = jnp.stack([inv_re * fold, -inv_im * fold], axis=3)
    upper, lower = lax.optimization_barrier(split_bf16(joined))
    form = "rnxhq,hcq->rnxc"
    scores = jnp.einsum(form, upper, table_hi, preferred_element_type=jnp.float32)
    scores = scores + jnp.einsum(form, lower, table_hi, preferred_element_type=jnp.float32)
    return scores + jnp.einsum(form, upper, table_lo, preferred_element_type=jnp.float32)


def gather_by_permutes(values, axis_name, count, here):
    blocks = [values]
    for shift in range(1, count):
        pairs = [(k, (k + shift) % count) for k in range(count)]
        blocks.append(lax.ppermute(values, axis_name, pairs))
    return blocks


def butterfly_max(values, axes, device_count):
    stride = 1
    while stride < device_count:
        radix = 4 if stride * 4 <= device_count else 2
        received = []
        for digit in range(1, radix):
            pairs = [(k, k ^ (digit * stride)) for k in range(device_count)]
            received.append(lax.ppermute(values, axes, pairs))
        for block in received:
            values = jnp.maximum(values, block)
        stride *= radix
    return values


def make_body(plane_count, inner_count, term_count):
    all_axes = ("plane", "inner", "term")

    def body(receptor_grids, term_weights, atom_weights, ligand_cells):
        terms_here, rows_here, cells = receptor_grids.shape
        rot_here = ligand_cells.shape[1]
        rot_total = rot_here * plane_count * inner_count
        plane = lax.axis_index("plane")
        inner = lax.axis_index("inner")
        term = lax.axis_index("term")
        own_rows = lax.all_gather(receptor_grids, "inner", axis=1, tiled=True)
        groups = gather_by_permutes(own_rows, "term", term_count, term)
        cell_blocks = gather_by_permutes(ligand_cells, "plane", plane_count, plane)
        cells_here = jnp.concatenate(cell_blocks, axis=1)
        share = cells_here.shape[1] // term_count
        voxels = lax.dynamic_slice_in_dim(cells_here, term * share, share, axis=1)
        local = term * share + jnp.arange(share, dtype=jnp.int32)
        source_plane = (plane - local // rot_here) % plane_count
        rot_ids = (source_plane * inner_count + inner) * rot_here + local % rot_here
        coefficients = atom_weights * term_weights[:, None]
        coefficients = jnp.concatenate(gather_by_permutes(coefficients, "term", term_count, term))
        with jax.named_scope("twiddle_tables"):
            factors = plane_factors()
            table_hi, table_lo = split_bf16(plane_table(factors, G))
            box_table = plane_table(factors, LB)
            tables = lax.optimization_barrier((box_table, table_hi, table_lo))
            box_table, table_hi, table_lo = tables
        with jax.named_scope("ligand_spectra"):
            lig_spec = ligand_spectra(voxels, coefficients, box_table)
        products = 0.0
        for index, grids in enumerate(groups):
            lo = index * terms_here
            with jax.named_scope("receptor_spectra"):
                rec_spec = receptor_mixed(grids, table_hi, table_lo)
            with jax.named_scope("correlate"):
                products = products + correlate(rec_spec, lig_spec[lo : lo + terms_here])
        with jax.named_scope("inverse_scores"):
            scores = inverse_scores(products, table_hi, table_lo)
            best_here = jnp.max(scores, axis=(2, 3))[0]
        receptors = plane_count
        columns = jnp.arange(rot_total, dtype=jnp.int32)
        hit = rot_ids[:, None] == columns[None, :]
        row = jnp.max(jnp.where(hit, best_here[:, None], -jnp.inf), axis=0)
        mine = jnp.arange(receptors, dtype=jnp.int32)[:, None] == plane
        placed = jnp.where(mine, row[None, :], -jnp.inf)
        placed = butterfly_max(placed, all_axes, plane_count * inner_count * term_count)
        start = (plane * inner_count + inner) * rot_here
        best_scores = lax.dynamic_slice_in_dim(placed, start, rot_here, axis=1)
        best_overall = jnp.max(placed, axis=1)
        return (best_scores, best_overall)

    return body


def solution(mesh):
    rot_count = mesh.shape["rot"]
    term_count = mesh.shape["term"]

    def run(receptor_grids, term_weights, atom_weights, ligand_cells):
        receptors = receptor_grids.shape[1] // G
        inner_count = rot_count // receptors
        devices = np.asarray(mesh.devices).reshape(receptors, inner_count, term_count)
        fine = jax.sharding.Mesh(devices, ("plane", "inner", "term"))
        rows = ("plane", "inner")
        placed = (P("term", rows, None), P("term"), P("term", None), P(None, rows, None))
        mapped = jax.shard_map(
            make_body(receptors, inner_count, term_count),
            mesh=fine,
            in_specs=placed,
            out_specs=(P(None, rows), P()),
            check_vma=False,
        )
        return mapped(receptor_grids, term_weights, atom_weights, ligand_cells)

    return run
```

```python
import math

import numpy as np

import jax
import jax.numpy as jnp
from jax import lax
from jax.sharding import PartitionSpec as P

G = 32
HZ = G // 2 + 1
LB = 16
WIDTH = 640

HIGH = lax.Precision.HIGH
HIGHEST = lax.Precision.HIGHEST


def line_table(freq_count, cell_count):
    freq = np.arange(freq_count)[:, None]
    cell = np.arange(cell_count)[None, :]
    phase = (freq * cell % G).astype(np.float64) * (2.0 * math.pi / G)
    return np.cos(phase).astype(np.float32), np.sin(phase).astype(np.float32)


def plane_factors():
    column = np.arange(2 * WIDTH)
    half = column // WIDTH
    freq = column % WIDTH
    valid = freq < G * HZ
    cell = np.arange(G)[:, None]
    phase_y = (cell * (freq // HZ)[None, :] % G) * (2.0 * math.pi / G)
    phase_z = (cell * (freq % HZ)[None, :] % G) * (2.0 * math.pi / G)
    cy, sy = np.cos(phase_y), np.sin(phase_y)
    cz, sz = np.cos(phase_z), np.sin(phase_z)
    first = np.where(half == 0, cy, sy) * valid
    third = np.where(half == 0, -sy, cy) * valid
    return [jnp.asarray(f.astype(np.float32)) for f in (first, cz, third, sz)]


def plane_table(factors, side):
    first, second, third, fourth = [
        jnp.transpose(f[:side].reshape(side, 2, WIDTH), (1, 0, 2)) for f in factors
    ]
    table = first[:, :, None, :] * second[:, None, :, :] + third[:, :, None, :] * fourth[:, None, :, :]
    return table.reshape(2, side * side, WIDTH)


def split_bf16(table):
    upper = lax.reduce_precision(table, exponent_bits=8, mantissa_bits=7)
    lower = table - upper
    return upper.astype(jnp.bfloat16), lower.astype(jnp.bfloat16)


def mix_tables(cell_count):
    cos_x, sin_x = line_table(G, cell_count)
    from_cos = np.concatenate([cos_x, -sin_x], axis=0)
    from_sin = np.concatenate([-sin_x, -cos_x], axis=0)
    return jnp.asarray(np.concatenate([from_cos, from_sin], axis=1))


def mix_table(cell_count):
    cos_x, sin_x = line_table(G, cell_count)
    return jnp.asarray(np.concatenate([cos_x, sin_x], axis=0))


def receptor_mixed(grids, table_hi, table_lo, mix):
    terms, rows, cells = grids.shape
    receptors = rows // G
    grids = grids.reshape(terms, receptors, G, cells)
    form = "trxc,hcq->trhxq"
    plane = jnp.einsum(form, grids, table_hi, preferred_element_type=jnp.float32)
    plane = plane + jnp.einsum(form, grids, table_lo, preferred_element_type=jnp.float32)
    plane = plane.reshape(terms, receptors, 2 * G, WIDTH)
    return jnp.einsum("pk,trkq->trpq", mix, plane, precision=HIGH)


def ligand_spectra(voxels, coefficients, box_table):
    yz_index = voxels[1] * LB + voxels[2]
    cells = jnp.arange(LB * LB, dtype=jnp.int32)
    onehot = (yz_index[:, :, None] == cells[None, None, :]).astype(jnp.bfloat16)
    x_cells = jnp.arange(LB, dtype=jnp.int32)
    in_x = (voxels[0][:, None, :] == x_cells[None, :, None]).astype(jnp.float32)
    weights = coefficients[None, :, None, :] * in_x[:, None, :, :]
    upper, lower = split_bf16(weights)
    form = "ntxa,nac->ntxc"
    grid = jnp.einsum(form, upper, onehot, preferred_element_type=jnp.float32)
    grid = grid + jnp.einsum(form, lower, onehot, preferred_element_type=jnp.float32)
    plane = jnp.einsum("ntxc,hcq->nthxq", grid, box_table, precision=HIGH)
    rot_count, terms = plane.shape[0], plane.shape[1]
    plane = plane.reshape(rot_count, terms, 2 * LB, WIDTH)
    return jnp.einsum("pk,ntkq->tnpq", mix_tables(LB), plane, precision=HIGH)


def correlate(rec_spec, lig_spec):
    rr = rec_spec[:, :, None, :G]
    ri = rec_spec[:, :, None, G:]
    lr = lig_spec[:, None, :, :G]
    li = lig_spec[:, None, :, G:]
    prod_re = jnp.sum(lr * rr + li * ri, axis=0)
    prod_im = jnp.sum(lr * ri - li * rr, axis=0)
    return jnp.stack([prod_re, prod_im], axis=0)


def inverse_scores(products, table_hi, table_lo):
    mixed = jnp.einsum("xp,srnpq->srnxq", mix_table(G), products, precision=HIGH)
    inv_re = mixed[0, :, :, :G] - mixed[1, :, :, G:]
    inv_im = mixed[1, :, :, :G] + mixed[0, :, :, G:]
    column = np.arange(WIDTH)
    freq_z = column % HZ
    fold = np.where((freq_z == 0) | (freq_z == G // 2), 1.0, 2.0) / float(G**3)
    fold = np.where(column < G * HZ, fold, 0.0)
    fold = jnp.asarray(fold.astype(np.float32))
    joined = jnp.stack([inv_re * fold, -inv_im * fold], axis=3)
    upper, lower = lax.optimization_barrier(split_bf16(joined))
    form = "rnxhq,hcq->rnxc"
    scores = jnp.einsum(form, upper, table_hi, preferred_element_type=jnp.float32)
    scores = scores + jnp.einsum(form, lower, table_hi, preferred_element_type=jnp.float32)
    return scores + jnp.einsum(form, upper, table_lo, preferred_element_type=jnp.float32)


def gather_by_permutes(values, axis_name, count, here):
    blocks = [values]
    for shift in range(1, count):
        pairs = [(k, (k + shift) % count) for k in range(count)]
        blocks.append(lax.ppermute(values, axis_name, pairs))
    return blocks


def butterfly_max(values, axes, device_count):
    stride = 1
    while stride < device_count:
        radix = 4 if stride * 4 <= device_count else 2
        received = []
        for digit in range(1, radix):
            pairs = [(k, k ^ (digit * stride)) for k in range(device_count)]
            received.append(lax.ppermute(values, axes, pairs))
        for block in received:
            values = jnp.maximum(values, block)
        stride *= radix
    return values


def make_body(plane_count, inner_count, term_count):
    all_axes = ("plane", "inner", "term")

    def body(receptor_grids, term_weights, atom_weights, ligand_cells):
        terms_here, rows_here, cells = receptor_grids.shape
        rot_here = ligand_cells.shape[1]
        rot_total = rot_here * plane_count * inner_count
        plane = lax.axis_index("plane")
        inner = lax.axis_index("inner")
        term = lax.axis_index("term")
        if inner_count <= 4:
            row_blocks = gather_by_permutes(receptor_grids, "inner", inner_count, inner)
            own_rows = jnp.concatenate(row_blocks, axis=1)
            slot_inner = (inner - jnp.arange(inner_count, dtype=jnp.int32)) % inner_count
        else:
            own_rows = lax.all_gather(receptor_grids, "inner", axis=1, tiled=True)
            slot_inner = jnp.arange(inner_count, dtype=jnp.int32)
        groups = gather_by_permutes(own_rows, "term", term_count, term)
        row_order = slot_inner[:, None] * rows_here + jnp.arange(rows_here, dtype=jnp.int32)
        row_order = row_order.reshape(-1)
        rec_mix = mix_tables(G)
        rec_mix = jnp.take(rec_mix, jnp.concatenate([row_order, row_order + G]), axis=1)
        cell_blocks = gather_by_permutes(ligand_cells, "plane", plane_count, plane)
        cells_here = jnp.concatenate(cell_blocks, axis=1)
        share = cells_here.shape[1] // term_count
        voxels = lax.dynamic_slice_in_dim(cells_here, term * share, share, axis=1)
        local = term * share + jnp.arange(share, dtype=jnp.int32)
        source_plane = (plane - local // rot_here) % plane_count
        rot_ids = (source_plane * inner_count + inner) * rot_here + local % rot_here
        coefficients = atom_weights * term_weights[:, None]
        coefficients = jnp.concatenate(gather_by_permutes(coefficients, "term", term_count, term))
        with jax.named_scope("twiddle_tables"):
            factors = plane_factors()
            table_hi, table_lo = split_bf16(plane_table(factors, G))
            box_table = plane_table(factors, LB)
            tables = lax.optimization_barrier((box_table, table_hi, table_lo))
            box_table, table_hi, table_lo = tables
        with jax.named_scope("ligand_spectra"):
            lig_spec = ligand_spectra(voxels, coefficients, box_table)
        products = 0.0
        for index, grids in enumerate(groups):
            lo = index * terms_here
            with jax.named_scope("receptor_spectra"):
                rec_spec = receptor_mixed(grids, table_hi, table_lo, rec_mix)
            with jax.named_scope("correlate"):
                products = products + correlate(rec_spec, lig_spec[lo : lo + terms_here])
        with jax.named_scope("inverse_scores"):
            scores = inverse_scores(products, table_hi, table_lo)
            best_here = jnp.max(scores, axis=(2, 3))[0]
        receptors = plane_count
        columns = jnp.arange(rot_total, dtype=jnp.int32)
        hit = rot_ids[:, None] == columns[None, :]
        row = jnp.max(jnp.where(hit, best_here[:, None], -jnp.inf), axis=0)
        mine = jnp.arange(receptors, dtype=jnp.int32)[:, None] == plane
        placed = jnp.where(mine, row[None, :], -jnp.inf)
        placed = butterfly_max(placed, all_axes, plane_count * inner_count * term_count)
        start = (plane * inner_count + inner) * rot_here
        best_scores = lax.dynamic_slice_in_dim(placed, start, rot_here, axis=1)
        best_overall = jnp.max(placed, axis=1)
        return (best_scores, best_overall)

    return body


def solution(mesh):
    rot_count = mesh.shape["rot"]
    term_count = mesh.shape["term"]

    def run(receptor_grids, term_weights, atom_weights, ligand_cells):
        receptors = receptor_grids.shape[1] // G
        inner_count = rot_count // receptors
        devices = np.asarray(mesh.devices).reshape(receptors, inner_count, term_count)
        fine = jax.sharding.Mesh(devices, ("plane", "inner", "term"))
        rows = ("plane", "inner")
        placed = (P("term", rows, None), P("term"), P("term", None), P(None, rows, None))
        mapped = jax.shard_map(
            make_body(receptors, inner_count, term_count),
            mesh=fine,
            in_specs=placed,
            out_specs=(P(None, rows), P()),
            check_vma=False,
        )
        return mapped(receptor_grids, term_weights, atom_weights, ligand_cells)

    return run
```

```python
import math

import numpy as np

import jax
import jax.numpy as jnp
from jax import lax
from jax.sharding import PartitionSpec as P

G = 32
HZ = G // 2 + 1
LB = 16
WIDTH = 640

HIGH = lax.Precision.HIGH
HIGHEST = lax.Precision.HIGHEST


def line_table(freq_count, cell_count):
    freq = np.arange(freq_count)[:, None]
    cell = np.arange(cell_count)[None, :]
    phase = (freq * cell % G).astype(np.float64) * (2.0 * math.pi / G)
    return np.cos(phase).astype(np.float32), np.sin(phase).astype(np.float32)


def plane_factors():
    column = np.arange(2 * WIDTH)
    half = column // WIDTH
    freq = column % WIDTH
    valid = freq < G * HZ
    cell = np.arange(G)[:, None]
    phase_y = (cell * (freq // HZ)[None, :] % G) * (2.0 * math.pi / G)
    phase_z = (cell * (freq % HZ)[None, :] % G) * (2.0 * math.pi / G)
    cy, sy = np.cos(phase_y), np.sin(phase_y)
    cz, sz = np.cos(phase_z), np.sin(phase_z)
    first = np.where(half == 0, cy, sy) * valid
    third = np.where(half == 0, -sy, cy) * valid
    return [jnp.asarray(f.astype(np.float32)) for f in (first, cz, third, sz)]


def plane_table(factors, side):
    first, second, third, fourth = [
        jnp.transpose(f[:side].reshape(side, 2, WIDTH), (1, 0, 2)) for f in factors
    ]
    table = first[:, :, None, :] * second[:, None, :, :] + third[:, :, None, :] * fourth[:, None, :, :]
    return table.reshape(2, side * side, WIDTH)


def split_bf16(table):
    upper = lax.reduce_precision(table, exponent_bits=8, mantissa_bits=7)
    lower = table - upper
    return upper.astype(jnp.bfloat16), lower.astype(jnp.bfloat16)


def mix_tables(cell_count):
    cos_x, sin_x = line_table(G, cell_count)
    from_cos = np.concatenate([cos_x, -sin_x], axis=0)
    from_sin = np.concatenate([-sin_x, -cos_x], axis=0)
    return jnp.asarray(np.concatenate([from_cos, from_sin], axis=1))


def mix_table(cell_count):
    cos_x, sin_x = line_table(G, cell_count)
    return jnp.asarray(np.concatenate([cos_x, sin_x], axis=0))


def receptor_mixed(grids, table_hi):
    terms, rows, cells = grids.shape
    receptors = rows // G
    grids = grids.reshape(terms, receptors, G, cells)
    plane = jnp.einsum("trxc,hcq->trhxq", grids, table_hi, preferred_element_type=jnp.float32)
    plane = plane.reshape(terms, receptors, 2 * G, WIDTH)
    return jnp.einsum("pk,trkq->trpq", mix_tables(G), plane, precision=HIGH)


def ligand_spectra(voxels, coefficients, box_table):
    yz_index = voxels[1] * LB + voxels[2]
    cells = jnp.arange(LB * LB, dtype=jnp.int32)
    onehot = (yz_index[:, :, None] == cells[None, None, :]).astype(jnp.bfloat16)
    x_cells = jnp.arange(LB, dtype=jnp.int32)
    in_x = (voxels[0][:, None, :] == x_cells[None, :, None]).astype(jnp.float32)
    weights = coefficients[None, :, None, :] * in_x[:, None, :, :]
    upper, lower = split_bf16(weights)
    form = "ntxa,nac->ntxc"
    grid = jnp.einsum(form, upper, onehot, preferred_element_type=jnp.float32)
    grid = grid + jnp.einsum(form, lower, onehot, preferred_element_type=jnp.float32)
    plane = jnp.einsum("ntxc,hcq->nthxq", grid, box_table, precision=HIGH)
    rot_count, terms = plane.shape[0], plane.shape[1]
    plane = plane.reshape(rot_count, terms, 2 * LB, WIDTH)
    return jnp.einsum("pk,ntkq->tnpq", mix_tables(LB), plane, precision=HIGH)


def correlate(rec_spec, lig_spec):
    rr = rec_spec[:, :, None, :G]
    ri = rec_spec[:, :, None, G:]
    lr = lig_spec[:, None, :, :G]
    li = lig_spec[:, None, :, G:]
    prod_re = jnp.sum(lr * rr + li * ri, axis=0)
    prod_im = jnp.sum(lr * ri - li * rr, axis=0)
    return jnp.stack([prod_re, prod_im], axis=0)


def inverse_scores(products, table_hi, table_lo):
    mixed = jnp.einsum("xp,srnpq->srnxq", mix_table(G), products, precision=HIGH)
    inv_re = mixed[0, :, :, :G] - mixed[1, :, :, G:]
    inv_im = mixed[1, :, :, :G] + mixed[0, :, :, G:]
    column = np.arange(WIDTH)
    freq_z = column % HZ
    fold = np.where((freq_z == 0) | (freq_z == G // 2), 1.0, 2.0) / float(G**3)
    fold = np.where(column < G * HZ, fold, 0.0)
    fold = jnp.asarray(fold.astype(np.float32))
    joined = jnp.stack([inv_re * fold, -inv_im * fold], axis=3)
    upper, lower = lax.optimization_barrier(split_bf16(joined))
    form = "rnxhq,hcq->rnxc"
    scores = jnp.einsum(form, upper, table_hi, preferred_element_type=jnp.float32)
    scores = scores + jnp.einsum(form, lower, table_hi, preferred_element_type=jnp.float32)
    return scores + jnp.einsum(form, upper, table_lo, preferred_element_type=jnp.float32)


def gather_by_permutes(values, axis_name, count, here):
    blocks = [values]
    for shift in range(1, count):
        pairs = [(k, (k + shift) % count) for k in range(count)]
        blocks.append(lax.ppermute(values, axis_name, pairs))
    return blocks


def butterfly_max(values, axes, device_count):
    stride = 1
    while stride < device_count:
        radix = 4 if stride * 4 <= device_count else 2
        received = []
        for digit in range(1, radix):
            pairs = [(k, k ^ (digit * stride)) for k in range(device_count)]
            received.append(lax.ppermute(values, axes, pairs))
        for block in received:
            values = jnp.maximum(values, block)
        stride *= radix
    return values


def make_body(plane_count, inner_count, term_count):
    all_axes = ("plane", "inner", "term")

    def body(receptor_grids, term_weights, atom_weights, ligand_cells):
        terms_here, rows_here, cells = receptor_grids.shape
        rot_here = ligand_cells.shape[1]
        rot_total = rot_here * plane_count * inner_count
        plane = lax.axis_index("plane")
        inner = lax.axis_index("inner")
        term = lax.axis_index("term")
        own_rows = lax.all_gather(receptor_grids, "inner", axis=1, tiled=True)
        groups = gather_by_permutes(own_rows, "term", term_count, term)
        cell_blocks = gather_by_permutes(ligand_cells, "plane", plane_count, plane)
        cells_here = jnp.concatenate(cell_blocks, axis=1)
        share = cells_here.shape[1] // term_count
        voxels = lax.dynamic_slice_in_dim(cells_here, term * share, share, axis=1)
        local = term * share + jnp.arange(share, dtype=jnp.int32)
        source_plane = (plane - local // rot_here) % plane_count
        rot_ids = (source_plane * inner_count + inner) * rot_here + local % rot_here
        coefficients = atom_weights * term_weights[:, None]
        coefficients = jnp.concatenate(gather_by_permutes(coefficients, "term", term_count, term))
        with jax.named_scope("twiddle_tables"):
            factors = plane_factors()
            table_hi, table_lo = split_bf16(plane_table(factors, G))
            box_table = plane_table(factors, LB)
            tables = lax.optimization_barrier((box_table, table_hi, table_lo))
            box_table, table_hi, table_lo = tables
        with jax.named_scope("ligand_spectra"):
            lig_spec = ligand_spectra(voxels, coefficients, box_table)
        products = 0.0
        for index, grids in enumerate(groups):
            lo = index * terms_here
            with jax.named_scope("receptor_spectra"):
                rec_spec = receptor_mixed(grids, table_hi)
            with jax.named_scope("correlate"):
                products = products + correlate(rec_spec, lig_spec[lo : lo + terms_here])
        with jax.named_scope("inverse_scores"):
            scores = inverse_scores(products, table_hi, table_lo)
            best_here = jnp.max(scores, axis=(2, 3))[0]
        receptors = plane_count
        columns = jnp.arange(rot_total, dtype=jnp.int32)
        hit = rot_ids[:, None] == columns[None, :]
        row = jnp.max(jnp.where(hit, best_here[:, None], -jnp.inf), axis=0)
        mine = jnp.arange(receptors, dtype=jnp.int32)[:, None] == plane
        placed = jnp.where(mine, row[None, :], -jnp.inf)
        placed = butterfly_max(placed, all_axes, plane_count * inner_count * term_count)
        start = (plane * inner_count + inner) * rot_here
        best_scores = lax.dynamic_slice_in_dim(placed, start, rot_here, axis=1)
        best_overall = jnp.max(placed, axis=1)
        return (best_scores, best_overall)

    return body


def solution(mesh):
    rot_count = mesh.shape["rot"]
    term_count = mesh.shape["term"]

    def run(receptor_grids, term_weights, atom_weights, ligand_cells):
        receptors = receptor_grids.shape[1] // G
        inner_count = rot_count // receptors
        devices = np.asarray(mesh.devices).reshape(receptors, inner_count, term_count)
        fine = jax.sharding.Mesh(devices, ("plane", "inner", "term"))
        rows = ("plane", "inner")
        placed = (P("term", rows, None), P("term"), P("term", None), P(None, rows, None))
        mapped = jax.shard_map(
            make_body(receptors, inner_count, term_count),
            mesh=fine,
            in_specs=placed,
            out_specs=(P(None, rows), P()),
            check_vma=False,
        )
        return mapped(receptor_grids, term_weights, atom_weights, ligand_cells)

    return run
```

```python
import math

import numpy as np

import jax
import jax.numpy as jnp
from jax import lax
from jax.sharding import PartitionSpec as P

G = 32
HZ = G // 2 + 1
LB = 16
WIDTH = 640

HIGH = lax.Precision.HIGH
HIGHEST = lax.Precision.HIGHEST


def line_table(freq_count, cell_count):
    freq = np.arange(freq_count)[:, None]
    cell = np.arange(cell_count)[None, :]
    phase = (freq * cell % G).astype(np.float64) * (2.0 * math.pi / G)
    return np.cos(phase).astype(np.float32), np.sin(phase).astype(np.float32)


def plane_factors():
    column = np.arange(2 * WIDTH)
    half = column // WIDTH
    freq = column % WIDTH
    valid = freq < G * HZ
    cell = np.arange(G)[:, None]
    phase_y = (cell * (freq // HZ)[None, :] % G) * (2.0 * math.pi / G)
    phase_z = (cell * (freq % HZ)[None, :] % G) * (2.0 * math.pi / G)
    cy, sy = np.cos(phase_y), np.sin(phase_y)
    cz, sz = np.cos(phase_z), np.sin(phase_z)
    first = np.where(half == 0, cy, sy) * valid
    third = np.where(half == 0, -sy, cy) * valid
    return [jnp.asarray(f.astype(np.float32)) for f in (first, cz, third, sz)]


def plane_table(factors, side):
    first, second, third, fourth = [
        jnp.transpose(f[:side].reshape(side, 2, WIDTH), (1, 0, 2)) for f in factors
    ]
    table = first[:, :, None, :] * second[:, None, :, :] + third[:, :, None, :] * fourth[:, None, :, :]
    return table.reshape(2, side * side, WIDTH)


def split_bf16(table):
    upper = lax.reduce_precision(table, exponent_bits=8, mantissa_bits=7)
    lower = table - upper
    return upper.astype(jnp.bfloat16), lower.astype(jnp.bfloat16)


def mix_tables(cell_count):
    cos_x, sin_x = line_table(G, cell_count)
    from_cos = np.concatenate([cos_x, -sin_x], axis=0)
    from_sin = np.concatenate([-sin_x, -cos_x], axis=0)
    return jnp.asarray(np.concatenate([from_cos, from_sin], axis=1))


def mix_table(cell_count):
    cos_x, sin_x = line_table(G, cell_count)
    return jnp.asarray(np.concatenate([cos_x, sin_x], axis=0))


def receptor_mixed(grids, table_hi):
    terms, rows, cells = grids.shape
    receptors = rows // G
    grids = grids.reshape(terms, receptors, G, cells)
    plane = jnp.einsum("trxc,hcq->trhxq", grids, table_hi, preferred_element_type=jnp.float32)
    plane = plane.reshape(terms, receptors, 2 * G, WIDTH)
    return jnp.einsum("pk,trkq->trpq", mix_tables(G), plane, precision=HIGH)


def ligand_spectra(voxels, coefficients, box_table):
    yz_index = voxels[1] * LB + voxels[2]
    cells = jnp.arange(LB * LB, dtype=jnp.int32)
    onehot = (yz_index[:, :, None] == cells[None, None, :]).astype(jnp.bfloat16)
    x_cells = jnp.arange(LB, dtype=jnp.int32)
    in_x = (voxels[0][:, None, :] == x_cells[None, :, None]).astype(jnp.float32)
    weights = coefficients[None, :, None, :] * in_x[:, None, :, :]
    upper, lower = split_bf16(weights)
    form = "ntxa,nac->ntxc"
    grid = jnp.einsum(form, upper, onehot, preferred_element_type=jnp.float32)
    grid = grid + jnp.einsum(form, lower, onehot, preferred_element_type=jnp.float32)
    plane = jnp.einsum("ntxc,hcq->nthxq", grid, box_table, precision=HIGH)
    rot_count, terms = plane.shape[0], plane.shape[1]
    plane = plane.reshape(rot_count, terms, 2 * LB, WIDTH)
    return jnp.einsum("pk,ntkq->tnpq", mix_tables(LB), plane, precision=HIGH)


def correlate(rec_spec, lig_spec):
    rr = rec_spec[:, :, None, :G]
    ri = rec_spec[:, :, None, G:]
    lr = lig_spec[:, None, :, :G]
    li = lig_spec[:, None, :, G:]
    prod_re = jnp.sum(lr * rr + li * ri, axis=0)
    prod_im = jnp.sum(lr * ri - li * rr, axis=0)
    return jnp.stack([prod_re, prod_im], axis=0)


def inverse_scores(products, table_hi, table_lo):
    mixed = jnp.einsum("xp,srnpq->srnxq", mix_table(G), products, precision=HIGH)
    inv_re = mixed[0, :, :, :G] - mixed[1, :, :, G:]
    inv_im = mixed[1, :, :, :G] + mixed[0, :, :, G:]
    column = np.arange(WIDTH)
    freq_z = column % HZ
    fold = np.where((freq_z == 0) | (freq_z == G // 2), 1.0, 2.0) / float(G**3)
    fold = np.where(column < G * HZ, fold, 0.0)
    fold = jnp.asarray(fold.astype(np.float32))
    joined = jnp.stack([inv_re * fold, -inv_im * fold], axis=3)
    upper, lower = lax.optimization_barrier(split_bf16(joined))
    form = "rnxhq,hcq->rnxc"
    scores = jnp.einsum(form, upper, table_hi, preferred_element_type=jnp.float32)
    scores = scores + jnp.einsum(form, lower, table_hi, preferred_element_type=jnp.float32)
    return scores + jnp.einsum(form, upper, table_lo, preferred_element_type=jnp.float32)


def gather_by_permutes(values, axis_name, count, here):
    blocks = [values]
    for shift in range(1, count):
        pairs = [(k, (k + shift) % count) for k in range(count)]
        blocks.append(lax.ppermute(values, axis_name, pairs))
    return blocks


def butterfly_max(values, axes, device_count):
    stride = 1
    while stride < device_count:
        radix = 4 if stride * 4 <= device_count else 2
        received = []
        for digit in range(1, radix):
            pairs = [(k, k ^ (digit * stride)) for k in range(device_count)]
            received.append(lax.ppermute(values, axes, pairs))
        for block in received:
            values = jnp.maximum(values, block)
        stride *= radix
    return values


def make_body(plane_count, inner_count, term_count):
    all_axes = ("plane", "inner", "term")

    def body(receptor_grids, term_weights, atom_weights, ligand_cells):
        terms_here, rows_here, cells = receptor_grids.shape
        rot_here = ligand_cells.shape[1]
        rot_total = rot_here * plane_count * inner_count
        plane = lax.axis_index("plane")
        inner = lax.axis_index("inner")
        term = lax.axis_index("term")
        own_rows = lax.all_gather(receptor_grids, "inner", axis=1, tiled=True)
        groups = gather_by_permutes(own_rows, "term", term_count, term)
        local_slots = jnp.arange(rot_here * plane_count, dtype=jnp.int32) // rot_here
        if plane_count & (plane_count - 1):
            cell_blocks = gather_by_permutes(ligand_cells, "plane", plane_count, plane)
            cells_here = jnp.concatenate(cell_blocks, axis=1)
            slot_plane = (plane - local_slots) % plane_count
        else:
            cells_here = ligand_cells
            shift = 1
            while shift < plane_count:
                pairs = [(k, k ^ shift) for k in range(plane_count)]
                moved = lax.ppermute(cells_here, "plane", pairs)
                cells_here = jnp.concatenate([cells_here, moved], axis=1)
                shift *= 2
            slot_plane = jnp.bitwise_xor(plane, local_slots)
        share = cells_here.shape[1] // term_count
        voxels = lax.dynamic_slice_in_dim(cells_here, term * share, share, axis=1)
        local = term * share + jnp.arange(share, dtype=jnp.int32)
        source_plane = lax.dynamic_slice_in_dim(slot_plane, term * share, share)
        rot_ids = (source_plane * inner_count + inner) * rot_here + local % rot_here
        coefficients = atom_weights * term_weights[:, None]
        coefficients = jnp.concatenate(gather_by_permutes(coefficients, "term", term_count, term))
        with jax.named_scope("twiddle_tables"):
            factors = plane_factors()
            table_hi, table_lo = split_bf16(plane_table(factors, G))
            box_table = plane_table(factors, LB)
            tables = lax.optimization_barrier((box_table, table_hi, table_lo))
            box_table, table_hi, table_lo = tables
        with jax.named_scope("ligand_spectra"):
            lig_spec = ligand_spectra(voxels, coefficients, box_table)
        products = 0.0
        for index, grids in enumerate(groups):
            lo = index * terms_here
            with jax.named_scope("receptor_spectra"):
                rec_spec = receptor_mixed(grids, table_hi)
            with jax.named_scope("correlate"):
                products = products + correlate(rec_spec, lig_spec[lo : lo + terms_here])
        with jax.named_scope("inverse_scores"):
            scores = inverse_scores(products, table_hi, table_lo)
            best_here = jnp.max(scores, axis=(2, 3))[0]
        receptors = plane_count
        columns = jnp.arange(rot_total, dtype=jnp.int32)
        hit = rot_ids[:, None] == columns[None, :]
        row = jnp.max(jnp.where(hit, best_here[:, None], -jnp.inf), axis=0)
        mine = jnp.arange(receptors, dtype=jnp.int32)[:, None] == plane
        placed = jnp.where(mine, row[None, :], -jnp.inf)
        placed = butterfly_max(placed, all_axes, plane_count * inner_count * term_count)
        start = (plane * inner_count + inner) * rot_here
        best_scores = lax.dynamic_slice_in_dim(placed, start, rot_here, axis=1)
        best_overall = jnp.max(placed, axis=1)
        return (best_scores, best_overall)

    return body


def solution(mesh):
    rot_count = mesh.shape["rot"]
    term_count = mesh.shape["term"]

    def run(receptor_grids, term_weights, atom_weights, ligand_cells):
        receptors = receptor_grids.shape[1] // G
        inner_count = rot_count // receptors
        devices = np.asarray(mesh.devices).reshape(receptors, inner_count, term_count)
        fine = jax.sharding.Mesh(devices, ("plane", "inner", "term"))
        rows = ("plane", "inner")
        placed = (P("term", rows, None), P("term"), P("term", None), P(None, rows, None))
        mapped = jax.shard_map(
            make_body(receptors, inner_count, term_count),
            mesh=fine,
            in_specs=placed,
            out_specs=(P(None, rows), P()),
            check_vma=False,
        )
        return mapped(receptor_grids, term_weights, atom_weights, ligand_cells)

    return run
```

```python
import math

import numpy as np

import jax
import jax.numpy as jnp
from jax import lax
from jax.sharding import PartitionSpec as P

G = 32
HZ = G // 2 + 1
LB = 16
WIDTH = 640

HIGH = lax.Precision.HIGH
HIGHEST = lax.Precision.HIGHEST


def line_table(freq_count, cell_count):
    freq = np.arange(freq_count)[:, None]
    cell = np.arange(cell_count)[None, :]
    phase = (freq * cell % G).astype(np.float64) * (2.0 * math.pi / G)
    return np.cos(phase).astype(np.float32), np.sin(phase).astype(np.float32)


def plane_factors():
    column = np.arange(2 * WIDTH)
    half = column // WIDTH
    freq = column % WIDTH
    valid = freq < G * HZ
    cell = np.arange(G)[:, None]
    phase_y = (cell * (freq // HZ)[None, :] % G) * (2.0 * math.pi / G)
    phase_z = (cell * (freq % HZ)[None, :] % G) * (2.0 * math.pi / G)
    cy, sy = np.cos(phase_y), np.sin(phase_y)
    cz, sz = np.cos(phase_z), np.sin(phase_z)
    first = np.where(half == 0, cy, sy) * valid
    third = np.where(half == 0, -sy, cy) * valid
    return [jnp.asarray(f.astype(np.float32)) for f in (first, cz, third, sz)]


def plane_table(factors, side):
    first, second, third, fourth = [
        jnp.transpose(f[:side].reshape(side, 2, WIDTH), (1, 0, 2)) for f in factors
    ]
    table = first[:, :, None, :] * second[:, None, :, :] + third[:, :, None, :] * fourth[:, None, :, :]
    return table.reshape(2, side * side, WIDTH)


def split_bf16(table):
    upper = lax.reduce_precision(table, exponent_bits=8, mantissa_bits=7)
    lower = table - upper
    return upper.astype(jnp.bfloat16), lower.astype(jnp.bfloat16)


def mix_tables(cell_count):
    cos_x, sin_x = line_table(G, cell_count)
    from_cos = np.concatenate([cos_x, -sin_x], axis=0)
    from_sin = np.concatenate([-sin_x, -cos_x], axis=0)
    return jnp.asarray(np.concatenate([from_cos, from_sin], axis=1))


def mix_table(cell_count):
    cos_x, sin_x = line_table(G, cell_count)
    return jnp.asarray(np.concatenate([cos_x, sin_x], axis=0))


def receptor_mixed(grids, table_hi):
    terms, rows, cells = grids.shape
    receptors = rows // G
    grids = grids.reshape(terms, receptors, G, cells)
    plane = jnp.einsum("trxc,hcq->trhxq", grids, table_hi, preferred_element_type=jnp.float32)
    plane = plane.reshape(terms, receptors, 2 * G, WIDTH)
    return jnp.einsum("pk,trkq->trpq", mix_tables(G), plane, precision=HIGH)


def ligand_spectra(voxels, coefficients, box_table):
    yz_index = voxels[1] * LB + voxels[2]
    cells = jnp.arange(LB * LB, dtype=jnp.int32)
    onehot = (yz_index[:, :, None] == cells[None, None, :]).astype(jnp.bfloat16)
    x_cells = jnp.arange(LB, dtype=jnp.int32)
    in_x = (voxels[0][:, None, :] == x_cells[None, :, None]).astype(jnp.float32)
    weights = coefficients[None, :, None, :] * in_x[:, None, :, :]
    upper, lower = split_bf16(weights)
    form = "ntxa,nac->ntxc"
    grid = jnp.einsum(form, upper, onehot, preferred_element_type=jnp.float32)
    grid = grid + jnp.einsum(form, lower, onehot, preferred_element_type=jnp.float32)
    plane = jnp.einsum("ntxc,hcq->nthxq", grid, box_table, precision=HIGH)
    rot_count, terms = plane.shape[0], plane.shape[1]
    plane = plane.reshape(rot_count, terms, 2 * LB, WIDTH)
    return jnp.einsum("pk,ntkq->tnpq", mix_tables(LB), plane, precision=HIGH)


def correlate(rec_spec, lig_spec):
    rr = rec_spec[:, :, None, :G]
    ri = rec_spec[:, :, None, G:]
    lr = lig_spec[:, None, :, :G]
    li = lig_spec[:, None, :, G:]
    prod_re = jnp.sum(lr * rr + li * ri, axis=0)
    prod_im = jnp.sum(lr * ri - li * rr, axis=0)
    return jnp.stack([prod_re, prod_im], axis=0)


def inverse_scores(products, table_hi, table_lo):
    mixed = jnp.einsum("xp,srnpq->srnxq", mix_table(G), products, precision=HIGH)
    inv_re = mixed[0, :, :, :G] - mixed[1, :, :, G:]
    inv_im = mixed[1, :, :, :G] + mixed[0, :, :, G:]
    column = np.arange(WIDTH)
    freq_z = column % HZ
    fold = np.where((freq_z == 0) | (freq_z == G // 2), 1.0, 2.0) / float(G**3)
    fold = np.where(column < G * HZ, fold, 0.0)
    fold = jnp.asarray(fold.astype(np.float32))
    joined = jnp.stack([inv_re * fold, -inv_im * fold], axis=3)
    upper, lower = lax.optimization_barrier(split_bf16(joined))
    form = "rnxhq,hcq->rnxc"
    scores = jnp.einsum(form, upper, table_hi, preferred_element_type=jnp.float32)
    scores = scores + jnp.einsum(form, lower, table_hi, preferred_element_type=jnp.float32)
    return scores + jnp.einsum(form, upper, table_lo, preferred_element_type=jnp.float32)


def gather_by_permutes(values, axis_name, count, here):
    blocks = [values]
    for shift in range(1, count):
        pairs = [(k, (k + shift) % count) for k in range(count)]
        blocks.append(lax.ppermute(values, axis_name, pairs))
    return blocks


def butterfly_max(values, axes, device_count):
    stride = 1
    while stride < device_count:
        radix = 4 if stride * 4 <= device_count else 2
        received = []
        for digit in range(1, radix):
            pairs = [(k, k ^ (digit * stride)) for k in range(device_count)]
            received.append(lax.ppermute(values, axes, pairs))
        for block in received:
            values = jnp.maximum(values, block)
        stride *= radix
    return values


def make_body(plane_count, inner_count, term_count):
    all_axes = ("plane", "inner", "term")

    def body(receptor_grids, term_weights, atom_weights, ligand_cells):
        terms_here, rows_here, cells = receptor_grids.shape
        rot_here = ligand_cells.shape[1]
        rot_total = rot_here * plane_count * inner_count
        plane = lax.axis_index("plane")
        inner = lax.axis_index("inner")
        term = lax.axis_index("term")
        own_rows = lax.all_gather(receptor_grids, "inner", axis=1, tiled=True)
        groups = gather_by_permutes(own_rows, "term", term_count, term)
        local_slots = jnp.arange(rot_here * plane_count, dtype=jnp.int32) // rot_here
        if plane_count & (plane_count - 1):
            cell_blocks = gather_by_permutes(ligand_cells, "plane", plane_count, plane)
            cells_here = jnp.concatenate(cell_blocks, axis=1)
            slot_plane = (plane - local_slots) % plane_count
        else:
            cells_here = ligand_cells
            shift = 1
            while shift < plane_count:
                pairs = [(k, k ^ shift) for k in range(plane_count)]
                moved = lax.ppermute(cells_here, "plane", pairs)
                cells_here = jnp.concatenate([cells_here, moved], axis=1)
                shift *= 2
            slot_plane = jnp.bitwise_xor(plane, local_slots)
        share = cells_here.shape[1] // term_count
        voxels = lax.dynamic_slice_in_dim(cells_here, term * share, share, axis=1)
        local = term * share + jnp.arange(share, dtype=jnp.int32)
        source_plane = lax.dynamic_slice_in_dim(slot_plane, term * share, share)
        rot_ids = (source_plane * inner_count + inner) * rot_here + local % rot_here
        coefficients = atom_weights * term_weights[:, None]
        coefficients = jnp.concatenate(gather_by_permutes(coefficients, "term", term_count, term))
        with jax.named_scope("twiddle_tables"):
            factors = plane_factors()
            full = plane_table(factors, G)
            table_hi = lax.reduce_precision(full, exponent_bits=8, mantissa_bits=7)
            table_lo = (plane_table(factors, G) - table_hi).astype(jnp.bfloat16)
            table_hi = table_hi.astype(jnp.bfloat16)
            table_hi, table_lo = lax.optimization_barrier((table_hi, table_lo))
            box_rows = table_hi.astype(jnp.float32) + table_lo.astype(jnp.float32)
            box_table = box_rows.reshape(2, G, G, WIDTH)[:, :LB, :LB].reshape(2, LB * LB, WIDTH)
        with jax.named_scope("ligand_spectra"):
            lig_spec = ligand_spectra(voxels, coefficients, box_table)
        products = 0.0
        for index, grids in enumerate(groups):
            lo = index * terms_here
            with jax.named_scope("receptor_spectra"):
                rec_spec = receptor_mixed(grids, table_hi)
            with jax.named_scope("correlate"):
                products = products + correlate(rec_spec, lig_spec[lo : lo + terms_here])
        with jax.named_scope("inverse_scores"):
            scores = inverse_scores(products, table_hi, table_lo)
            best_here = jnp.max(scores, axis=(2, 3))[0]
        receptors = plane_count
        columns = jnp.arange(rot_total, dtype=jnp.int32)
        hit = rot_ids[:, None] == columns[None, :]
        row = jnp.max(jnp.where(hit, best_here[:, None], -jnp.inf), axis=0)
        mine = jnp.arange(receptors, dtype=jnp.int32)[:, None] == plane
        placed = jnp.where(mine, row[None, :], -jnp.inf)
        placed = butterfly_max(placed, all_axes, plane_count * inner_count * term_count)
        start = (plane * inner_count + inner) * rot_here
        best_scores = lax.dynamic_slice_in_dim(placed, start, rot_here, axis=1)
        best_overall = jnp.max(placed, axis=1)
        return (best_scores, best_overall)

    return body


def solution(mesh):
    rot_count = mesh.shape["rot"]
    term_count = mesh.shape["term"]

    def run(receptor_grids, term_weights, atom_weights, ligand_cells):
        receptors = receptor_grids.shape[1] // G
        inner_count = rot_count // receptors
        devices = np.asarray(mesh.devices).reshape(receptors, inner_count, term_count)
        fine = jax.sharding.Mesh(devices, ("plane", "inner", "term"))
        rows = ("plane", "inner")
        placed = (P("term", rows, None), P("term"), P("term", None), P(None, rows, None))
        mapped = jax.shard_map(
            make_body(receptors, inner_count, term_count),
            mesh=fine,
            in_specs=placed,
            out_specs=(P(None, rows), P()),
            check_vma=False,
        )
        return mapped(receptor_grids, term_weights, atom_weights, ligand_cells)

    return run
```

```python
import math

import numpy as np

import jax
import jax.numpy as jnp
from jax import lax
from jax.sharding import PartitionSpec as P

G = 32
HZ = G // 2 + 1
LB = 16
WIDTH = 640

HIGH = lax.Precision.HIGH
HIGHEST = lax.Precision.HIGHEST


def line_table(freq_count, cell_count):
    freq = np.arange(freq_count)[:, None]
    cell = np.arange(cell_count)[None, :]
    phase = (freq * cell % G).astype(np.float64) * (2.0 * math.pi / G)
    return np.cos(phase).astype(np.float32), np.sin(phase).astype(np.float32)


def plane_factors():
    column = np.arange(2 * WIDTH)
    half = column // WIDTH
    freq = column % WIDTH
    valid = freq < G * HZ
    cell = np.arange(G)[:, None]
    phase_y = (cell * (freq // HZ)[None, :] % G) * (2.0 * math.pi / G)
    phase_z = (cell * (freq % HZ)[None, :] % G) * (2.0 * math.pi / G)
    cy, sy = np.cos(phase_y), np.sin(phase_y)
    cz, sz = np.cos(phase_z), np.sin(phase_z)
    first = np.where(half == 0, cy, sy) * valid
    third = np.where(half == 0, -sy, cy) * valid
    return [jnp.asarray(f.astype(np.float32)) for f in (first, cz, third, sz)]


def plane_table(factors, side):
    first, second, third, fourth = [
        jnp.transpose(f[:side].reshape(side, 2, WIDTH), (1, 0, 2)) for f in factors
    ]
    table = first[:, :, None, :] * second[:, None, :, :] + third[:, :, None, :] * fourth[:, None, :, :]
    return table.reshape(2, side * side, WIDTH)


def split_bf16(table):
    upper = lax.reduce_precision(table, exponent_bits=8, mantissa_bits=7)
    lower = table - upper
    return upper.astype(jnp.bfloat16), lower.astype(jnp.bfloat16)


def mix_tables(cell_count):
    cos_x, sin_x = line_table(G, cell_count)
    from_cos = np.concatenate([cos_x, -sin_x], axis=0)
    from_sin = np.concatenate([-sin_x, -cos_x], axis=0)
    return jnp.asarray(np.concatenate([from_cos, from_sin], axis=1))


def mix_table(cell_count):
    cos_x, sin_x = line_table(G, cell_count)
    return jnp.asarray(np.concatenate([cos_x, sin_x], axis=0))


def receptor_mixed(grids, table_hi):
    terms, rows, cells = grids.shape
    receptors = rows // G
    grids = grids.reshape(terms, receptors, G, cells)
    plane = jnp.einsum("trxc,hcq->trhxq", grids, table_hi, preferred_element_type=jnp.float32)
    plane = plane.reshape(terms, receptors, 2 * G, WIDTH)
    return jnp.einsum("pk,trkq->trpq", mix_tables(G), plane, precision=HIGH)


def ligand_spectra(voxels, coefficients, box_table):
    yz_index = voxels[1] * LB + voxels[2]
    cells = jnp.arange(LB * LB, dtype=jnp.int32)
    onehot = (yz_index[:, :, None] == cells[None, None, :]).astype(jnp.bfloat16)
    x_cells = jnp.arange(LB, dtype=jnp.int32)
    in_x = (voxels[0][:, None, :] == x_cells[None, :, None]).astype(jnp.float32)
    weights = coefficients[None, :, None, :] * in_x[:, None, :, :]
    upper, lower = split_bf16(weights)
    terms = upper.shape[1]
    both = jnp.concatenate([upper, lower], axis=1)
    both = jnp.einsum("ntxa,nac->ntxc", both, onehot, preferred_element_type=jnp.float32)
    grid = both[:, :terms] + both[:, terms:]
    plane = jnp.einsum("ntxc,hcq->nthxq", grid, box_table, precision=HIGH)
    rot_count, terms = plane.shape[0], plane.shape[1]
    plane = plane.reshape(rot_count, terms, 2 * LB, WIDTH)
    return jnp.einsum("pk,ntkq->tnpq", mix_tables(LB), plane, precision=HIGH)


def correlate(rec_spec, lig_spec):
    rr = rec_spec[:, :, None, :G]
    ri = rec_spec[:, :, None, G:]
    lr = lig_spec[:, None, :, :G]
    li = lig_spec[:, None, :, G:]
    prod_re = jnp.sum(lr * rr + li * ri, axis=0)
    prod_im = jnp.sum(lr * ri - li * rr, axis=0)
    return jnp.stack([prod_re, prod_im], axis=0)


def inverse_scores(products, table_hi, table_lo):
    mixed = jnp.einsum("xp,srnpq->srnxq", mix_table(G), products, precision=HIGH)
    inv_re = mixed[0, :, :, :G] - mixed[1, :, :, G:]
    inv_im = mixed[1, :, :, :G] + mixed[0, :, :, G:]
    column = np.arange(WIDTH)
    freq_z = column % HZ
    fold = np.where((freq_z == 0) | (freq_z == G // 2), 1.0, 2.0) / float(G**3)
    fold = np.where(column < G * HZ, fold, 0.0)
    fold = jnp.asarray(fold.astype(np.float32))
    joined = jnp.stack([inv_re * fold, -inv_im * fold], axis=3)
    upper, lower = lax.optimization_barrier(split_bf16(joined))
    form = "rnxhq,hcq->rnxc"
    count = upper.shape[0]
    both = jnp.concatenate([upper, lower], axis=0)
    both = jnp.einsum(form, both, table_hi, preferred_element_type=jnp.float32)
    scores = both[:count] + both[count:]
    return scores + jnp.einsum(form, upper, table_lo, preferred_element_type=jnp.float32)


def gather_by_permutes(values, axis_name, count, here):
    blocks = [values]
    for shift in range(1, count):
        pairs = [(k, (k + shift) % count) for k in range(count)]
        blocks.append(lax.ppermute(values, axis_name, pairs))
    return blocks


def butterfly_max(values, axes, device_count):
    stride = 1
    while stride < device_count:
        radix = 4 if stride * 4 <= device_count else 2
        received = []
        for digit in range(1, radix):
            pairs = [(k, k ^ (digit * stride)) for k in range(device_count)]
            received.append(lax.ppermute(values, axes, pairs))
        for block in received:
            values = jnp.maximum(values, block)
        stride *= radix
    return values


def make_body(plane_count, inner_count, term_count):
    all_axes = ("plane", "inner", "term")

    def body(receptor_grids, term_weights, atom_weights, ligand_cells):
        terms_here, rows_here, cells = receptor_grids.shape
        rot_here = ligand_cells.shape[1]
        rot_total = rot_here * plane_count * inner_count
        plane = lax.axis_index("plane")
        inner = lax.axis_index("inner")
        term = lax.axis_index("term")
        own_rows = lax.all_gather(receptor_grids, "inner", axis=1, tiled=True)
        groups = gather_by_permutes(own_rows, "term", term_count, term)
        local_slots = jnp.arange(rot_here * plane_count, dtype=jnp.int32) // rot_here
        if plane_count & (plane_count - 1):
            cell_blocks = gather_by_permutes(ligand_cells, "plane", plane_count, plane)
            cells_here = jnp.concatenate(cell_blocks, axis=1)
            slot_plane = (plane - local_slots) % plane_count
        else:
            cells_here = ligand_cells
            shift = 1
            while shift < plane_count:
                pairs = [(k, k ^ shift) for k in range(plane_count)]
                moved = lax.ppermute(cells_here, "plane", pairs)
                cells_here = jnp.concatenate([cells_here, moved], axis=1)
                shift *= 2
            slot_plane = jnp.bitwise_xor(plane, local_slots)
        share = cells_here.shape[1] // term_count
        voxels = lax.dynamic_slice_in_dim(cells_here, term * share, share, axis=1)
        local = term * share + jnp.arange(share, dtype=jnp.int32)
        source_plane = lax.dynamic_slice_in_dim(slot_plane, term * share, share)
        rot_ids = (source_plane * inner_count + inner) * rot_here + local % rot_here
        coefficients = atom_weights * term_weights[:, None]
        coefficients = jnp.concatenate(gather_by_permutes(coefficients, "term", term_count, term))
        with jax.named_scope("twiddle_tables"):
            factors = plane_factors()
            table_hi, table_lo = split_bf16(plane_table(factors, G))
            box_table = plane_table(factors, LB)
            tables = lax.optimization_barrier((box_table, table_hi, table_lo))
            box_table, table_hi, table_lo = tables
        with jax.named_scope("ligand_spectra"):
            lig_spec = ligand_spectra(voxels, coefficients, box_table)
        products = 0.0
        for index, grids in enumerate(groups):
            lo = index * terms_here
            with jax.named_scope("receptor_spectra"):
                rec_spec = receptor_mixed(grids, table_hi)
            with jax.named_scope("correlate"):
                products = products + correlate(rec_spec, lig_spec[lo : lo + terms_here])
        with jax.named_scope("inverse_scores"):
            scores = inverse_scores(products, table_hi, table_lo)
            best_here = jnp.max(scores, axis=(2, 3))[0]
        receptors = plane_count
        columns = jnp.arange(rot_total, dtype=jnp.int32)
        hit = rot_ids[:, None] == columns[None, :]
        row = jnp.max(jnp.where(hit, best_here[:, None], -jnp.inf), axis=0)
        mine = jnp.arange(receptors, dtype=jnp.int32)[:, None] == plane
        placed = jnp.where(mine, row[None, :], -jnp.inf)
        placed = butterfly_max(placed, all_axes, plane_count * inner_count * term_count)
        start = (plane * inner_count + inner) * rot_here
        best_scores = lax.dynamic_slice_in_dim(placed, start, rot_here, axis=1)
        best_overall = jnp.max(placed, axis=1)
        return (best_scores, best_overall)

    return body


def solution(mesh):
    rot_count = mesh.shape["rot"]
    term_count = mesh.shape["term"]

    def run(receptor_grids, term_weights, atom_weights, ligand_cells):
        receptors = receptor_grids.shape[1] // G
        inner_count = rot_count // receptors
        devices = np.asarray(mesh.devices).reshape(receptors, inner_count, term_count)
        fine = jax.sharding.Mesh(devices, ("plane", "inner", "term"))
        rows = ("plane", "inner")
        placed = (P("term", rows, None), P("term"), P("term", None), P(None, rows, None))
        mapped = jax.shard_map(
            make_body(receptors, inner_count, term_count),
            mesh=fine,
            in_specs=placed,
            out_specs=(P(None, rows), P()),
            check_vma=False,
        )
        return mapped(receptor_grids, term_weights, atom_weights, ligand_cells)

    return run
```

```python
import math

import numpy as np

import jax
import jax.numpy as jnp
from jax import lax
from jax.sharding import PartitionSpec as P

G = 32
HZ = G // 2 + 1
LB = 16
WIDTH = 640

HIGH = lax.Precision.HIGH
HIGHEST = lax.Precision.HIGHEST


def line_table(freq_count, cell_count):
    freq = np.arange(freq_count)[:, None]
    cell = np.arange(cell_count)[None, :]
    phase = (freq * cell % G).astype(np.float64) * (2.0 * math.pi / G)
    return np.cos(phase).astype(np.float32), np.sin(phase).astype(np.float32)


def plane_factors():
    column = np.arange(2 * WIDTH)
    half = column // WIDTH
    freq = column % WIDTH
    valid = freq < G * HZ
    cell = np.arange(G)[:, None]
    phase_y = (cell * (freq // HZ)[None, :] % G) * (2.0 * math.pi / G)
    phase_z = (cell * (freq % HZ)[None, :] % G) * (2.0 * math.pi / G)
    cy, sy = np.cos(phase_y), np.sin(phase_y)
    cz, sz = np.cos(phase_z), np.sin(phase_z)
    first = np.where(half == 0, cy, sy) * valid
    third = np.where(half == 0, -sy, cy) * valid
    return [jnp.asarray(f.astype(np.float32)) for f in (first, cz, third, sz)]


def plane_table(factors, side):
    first, second, third, fourth = [
        jnp.transpose(f[:side].reshape(side, 2, WIDTH), (1, 0, 2)) for f in factors
    ]
    table = first[:, :, None, :] * second[:, None, :, :] + third[:, :, None, :] * fourth[:, None, :, :]
    return table.reshape(2, side * side, WIDTH)


def split_bf16(table):
    upper = lax.reduce_precision(table, exponent_bits=8, mantissa_bits=7)
    lower = table - upper
    return upper.astype(jnp.bfloat16), lower.astype(jnp.bfloat16)


def mix_tables(cell_count):
    cos_x, sin_x = line_table(G, cell_count)
    from_cos = np.concatenate([cos_x, -sin_x], axis=0)
    from_sin = np.concatenate([-sin_x, -cos_x], axis=0)
    return jnp.asarray(np.concatenate([from_cos, from_sin], axis=1))


def mix_table(cell_count):
    cos_x, sin_x = line_table(G, cell_count)
    return jnp.asarray(np.concatenate([cos_x, sin_x], axis=0))


def receptor_mixed(grids, table_hi):
    terms, rows, cells = grids.shape
    receptors = rows // G
    grids = grids.reshape(terms, receptors, G, cells)
    plane = jnp.einsum("trxc,hcq->trhxq", grids, table_hi, preferred_element_type=jnp.float32)
    plane = plane.reshape(terms, receptors, 2 * G, WIDTH)
    return jnp.einsum("pk,trkq->trpq", mix_tables(G), plane, precision=HIGH)


def ligand_spectra(voxels, coefficients, box_table):
    yz_index = voxels[1] * LB + voxels[2]
    cells = jnp.arange(LB * LB, dtype=jnp.int32)
    onehot = (yz_index[:, :, None] == cells[None, None, :]).astype(jnp.bfloat16)
    x_cells = jnp.arange(LB, dtype=jnp.int32)
    in_x = (voxels[0][:, None, :] == x_cells[None, :, None]).astype(jnp.float32)
    weights = coefficients[None, :, None, :] * in_x[:, None, :, :]
    upper, lower = split_bf16(weights)
    form = "ntxa,nac->ntxc"
    grid = jnp.einsum(form, upper, onehot, preferred_element_type=jnp.float32)
    grid = grid + jnp.einsum(form, lower, onehot, preferred_element_type=jnp.float32)
    plane = jnp.einsum("ntxc,hcq->nthxq", grid, box_table, precision=HIGH)
    rot_count, terms = plane.shape[0], plane.shape[1]
    plane = plane.reshape(rot_count, terms, 2 * LB, WIDTH)
    return jnp.einsum("pk,ntkq->tnpq", mix_tables(LB), plane, precision=HIGH)


def correlate(rec_spec, lig_spec):
    rr = rec_spec[:, :, None, :G]
    ri = rec_spec[:, :, None, G:]
    lr = lig_spec[:, None, :, :G]
    li = lig_spec[:, None, :, G:]
    prod_re = jnp.sum(lr * rr + li * ri, axis=0)
    prod_im = jnp.sum(lr * ri - li * rr, axis=0)
    return jnp.stack([prod_re, prod_im], axis=0)


def inverse_scores(products, table_hi, table_lo):
    mixed = jnp.einsum("xp,srnpq->srnxq", mix_table(G), products, precision=HIGH)
    inv_re = mixed[0, :, :, :G] - mixed[1, :, :, G:]
    inv_im = mixed[1, :, :, :G] + mixed[0, :, :, G:]
    column = np.arange(WIDTH)
    freq_z = column % HZ
    fold = np.where((freq_z == 0) | (freq_z == G // 2), 1.0, 2.0) / float(G**3)
    fold = np.where(column < G * HZ, fold, 0.0)
    fold = jnp.asarray(fold.astype(np.float32))
    joined = jnp.stack([inv_re * fold, -inv_im * fold], axis=3)
    upper, lower = lax.optimization_barrier(split_bf16(joined))
    form = "rnxhq,hcq->rnxc"
    scores = jnp.einsum(form, upper, table_hi, preferred_element_type=jnp.float32)
    scores = scores + jnp.einsum(form, lower, table_hi, preferred_element_type=jnp.float32)
    return scores + jnp.einsum(form, upper, table_lo, preferred_element_type=jnp.float32)


def gather_by_permutes(values, axis_name, count, here):
    blocks = [values]
    for shift in range(1, count):
        pairs = [(k, (k + shift) % count) for k in range(count)]
        blocks.append(lax.ppermute(values, axis_name, pairs))
    return blocks


def butterfly_max(values, axes, device_count):
    stride = 1
    while stride < device_count:
        radix = 2
        received = []
        for digit in range(1, radix):
            pairs = [(k, k ^ (digit * stride)) for k in range(device_count)]
            received.append(lax.ppermute(values, axes, pairs))
        for block in received:
            values = jnp.maximum(values, block)
        stride *= radix
    return values


def make_body(plane_count, inner_count, term_count):
    all_axes = ("plane", "inner", "term")

    def body(receptor_grids, term_weights, atom_weights, ligand_cells):
        terms_here, rows_here, cells = receptor_grids.shape
        rot_here = ligand_cells.shape[1]
        rot_total = rot_here * plane_count * inner_count
        plane = lax.axis_index("plane")
        inner = lax.axis_index("inner")
        term = lax.axis_index("term")
        own_rows = lax.all_gather(receptor_grids, "inner", axis=1, tiled=True)
        groups = gather_by_permutes(own_rows, "term", term_count, term)
        local_slots = jnp.arange(rot_here * plane_count, dtype=jnp.int32) // rot_here
        if plane_count & (plane_count - 1):
            cell_blocks = gather_by_permutes(ligand_cells, "plane", plane_count, plane)
            cells_here = jnp.concatenate(cell_blocks, axis=1)
            slot_plane = (plane - local_slots) % plane_count
        else:
            cells_here = ligand_cells
            shift = 1
            while shift < plane_count:
                pairs = [(k, k ^ shift) for k in range(plane_count)]
                moved = lax.ppermute(cells_here, "plane", pairs)
                cells_here = jnp.concatenate([cells_here, moved], axis=1)
                shift *= 2
            slot_plane = jnp.bitwise_xor(plane, local_slots)
        share = cells_here.shape[1] // term_count
        voxels = lax.dynamic_slice_in_dim(cells_here, term * share, share, axis=1)
        local = term * share + jnp.arange(share, dtype=jnp.int32)
        source_plane = lax.dynamic_slice_in_dim(slot_plane, term * share, share)
        rot_ids = (source_plane * inner_count + inner) * rot_here + local % rot_here
        coefficients = atom_weights * term_weights[:, None]
        coefficients = jnp.concatenate(gather_by_permutes(coefficients, "term", term_count, term))
        with jax.named_scope("twiddle_tables"):
            factors = plane_factors()
            table_hi, table_lo = split_bf16(plane_table(factors, G))
            box_table = plane_table(factors, LB)
            tables = lax.optimization_barrier((box_table, table_hi, table_lo))
            box_table, table_hi, table_lo = tables
        with jax.named_scope("ligand_spectra"):
            lig_spec = ligand_spectra(voxels, coefficients, box_table)
        products = 0.0
        for index, grids in enumerate(groups):
            lo = index * terms_here
            with jax.named_scope("receptor_spectra"):
                rec_spec = receptor_mixed(grids, table_hi)
            with jax.named_scope("correlate"):
                products = products + correlate(rec_spec, lig_spec[lo : lo + terms_here])
        with jax.named_scope("inverse_scores"):
            scores = inverse_scores(products, table_hi, table_lo)
            best_here = jnp.max(scores, axis=(2, 3))[0]
        receptors = plane_count
        columns = jnp.arange(rot_total, dtype=jnp.int32)
        hit = rot_ids[:, None] == columns[None, :]
        row = jnp.max(jnp.where(hit, best_here[:, None], -jnp.inf), axis=0)
        mine = jnp.arange(receptors, dtype=jnp.int32)[:, None] == plane
        placed = jnp.where(mine, row[None, :], -jnp.inf)
        placed = butterfly_max(placed, all_axes, plane_count * inner_count * term_count)
        start = (plane * inner_count + inner) * rot_here
        best_scores = lax.dynamic_slice_in_dim(placed, start, rot_here, axis=1)
        best_overall = jnp.max(placed, axis=1)
        return (best_scores, best_overall)

    return body


def solution(mesh):
    rot_count = mesh.shape["rot"]
    term_count = mesh.shape["term"]

    def run(receptor_grids, term_weights, atom_weights, ligand_cells):
        receptors = receptor_grids.shape[1] // G
        inner_count = rot_count // receptors
        devices = np.asarray(mesh.devices).reshape(receptors, inner_count, term_count)
        fine = jax.sharding.Mesh(devices, ("plane", "inner", "term"))
        rows = ("plane", "inner")
        placed = (P("term", rows, None), P("term"), P("term", None), P(None, rows, None))
        mapped = jax.shard_map(
            make_body(receptors, inner_count, term_count),
            mesh=fine,
            in_specs=placed,
            out_specs=(P(None, rows), P()),
            check_vma=False,
        )
        return mapped(receptor_grids, term_weights, atom_weights, ligand_cells)

    return run
```

```python
import math

import numpy as np

import jax
import jax.numpy as jnp
from jax import lax
from jax.sharding import PartitionSpec as P

G = 32
HZ = G // 2 + 1
LB = 16
WIDTH = 640

HIGH = lax.Precision.HIGH
HIGHEST = lax.Precision.HIGHEST


def line_table(freq_count, cell_count):
    freq = np.arange(freq_count)[:, None]
    cell = np.arange(cell_count)[None, :]
    phase = (freq * cell % G).astype(np.float64) * (2.0 * math.pi / G)
    return np.cos(phase).astype(np.float32), np.sin(phase).astype(np.float32)


def plane_factors():
    column = np.arange(2 * WIDTH)
    half = column // WIDTH
    freq = column % WIDTH
    valid = freq < G * HZ
    cell = np.arange(G)[:, None]
    phase_y = (cell * (freq // HZ)[None, :] % G) * (2.0 * math.pi / G)
    phase_z = (cell * (freq % HZ)[None, :] % G) * (2.0 * math.pi / G)
    cy, sy = np.cos(phase_y), np.sin(phase_y)
    cz, sz = np.cos(phase_z), np.sin(phase_z)
    first = np.where(half == 0, cy, sy) * valid
    third = np.where(half == 0, -sy, cy) * valid
    return [jnp.asarray(f.astype(np.float32)) for f in (first, cz, third, sz)]


def plane_table(factors, side):
    first, second, third, fourth = [
        jnp.transpose(f[:side].reshape(side, 2, WIDTH), (1, 0, 2)) for f in factors
    ]
    table = first[:, :, None, :] * second[:, None, :, :] + third[:, :, None, :] * fourth[:, None, :, :]
    return table.reshape(2, side * side, WIDTH)


def split_bf16(table):
    upper = lax.reduce_precision(table, exponent_bits=8, mantissa_bits=7)
    lower = table - upper
    return upper.astype(jnp.bfloat16), lower.astype(jnp.bfloat16)


def mix_tables(cell_count):
    cos_x, sin_x = line_table(G, cell_count)
    from_cos = np.concatenate([cos_x, -sin_x], axis=0)
    from_sin = np.concatenate([-sin_x, -cos_x], axis=0)
    return jnp.asarray(np.concatenate([from_cos, from_sin], axis=1))


def mix_table(cell_count):
    cos_x, sin_x = line_table(G, cell_count)
    return jnp.asarray(np.concatenate([cos_x, sin_x], axis=0))


def receptor_mixed(grids, table_hi):
    terms, rows, cells = grids.shape
    receptors = rows // G
    grids = grids.reshape(terms, receptors, G, cells)
    plane = jnp.einsum("trxc,hcq->trhxq", grids, table_hi, preferred_element_type=jnp.float32)
    plane = plane.reshape(terms, receptors, 2 * G, WIDTH)
    return jnp.einsum("pk,trkq->trpq", mix_tables(G), plane, precision=HIGH)


def ligand_spectra(voxels, coefficients, box_table):
    yz_index = voxels[1] * LB + voxels[2]
    cells = jnp.arange(LB * LB, dtype=jnp.int32)
    onehot = (yz_index[:, :, None] == cells[None, None, :]).astype(jnp.bfloat16)
    x_cells = jnp.arange(LB, dtype=jnp.int32)
    in_x = (voxels[0][:, None, :] == x_cells[None, :, None]).astype(jnp.float32)
    weights = coefficients[None, :, None, :] * in_x[:, None, :, :]
    upper, lower = split_bf16(weights)
    form = "ntxa,nac->ntxc"
    grid = jnp.einsum(form, upper, onehot, preferred_element_type=jnp.float32)
    grid = grid + jnp.einsum(form, lower, onehot, preferred_element_type=jnp.float32)
    plane = jnp.einsum("ntxc,hcq->nthxq", grid, box_table, precision=HIGH)
    rot_count, terms = plane.shape[0], plane.shape[1]
    plane = plane.reshape(rot_count, terms, 2 * LB, WIDTH)
    return jnp.einsum("pk,ntkq->ntpq", mix_tables(LB), plane, precision=HIGH)


def correlate(rec_spec, lig_spec):
    rr = rec_spec[None, :, 0, :G]
    ri = rec_spec[None, :, 0, G:]
    lr = lig_spec[:, :, :G]
    li = lig_spec[:, :, G:]
    prod_re = jnp.sum(lr * rr + li * ri, axis=1)
    prod_im = jnp.sum(lr * ri - li * rr, axis=1)
    return jnp.stack([prod_re, prod_im], axis=0)[:, None]


def inverse_scores(products, table_hi, table_lo):
    mixed = jnp.einsum("xp,srnpq->srnxq", mix_table(G), products, precision=HIGH)
    inv_re = mixed[0, :, :, :G] - mixed[1, :, :, G:]
    inv_im = mixed[1, :, :, :G] + mixed[0, :, :, G:]
    column = np.arange(WIDTH)
    freq_z = column % HZ
    fold = np.where((freq_z == 0) | (freq_z == G // 2), 1.0, 2.0) / float(G**3)
    fold = np.where(column < G * HZ, fold, 0.0)
    fold = jnp.asarray(fold.astype(np.float32))
    joined = jnp.stack([inv_re * fold, -inv_im * fold], axis=3)
    upper, lower = lax.optimization_barrier(split_bf16(joined))
    form = "rnxhq,hcq->rnxc"
    scores = jnp.einsum(form, upper, table_hi, preferred_element_type=jnp.float32)
    scores = scores + jnp.einsum(form, lower, table_hi, preferred_element_type=jnp.float32)
    return scores + jnp.einsum(form, upper, table_lo, preferred_element_type=jnp.float32)


def gather_by_permutes(values, axis_name, count, here):
    blocks = [values]
    for shift in range(1, count):
        pairs = [(k, (k + shift) % count) for k in range(count)]
        blocks.append(lax.ppermute(values, axis_name, pairs))
    return blocks


def butterfly_max(values, axes, device_count):
    stride = 1
    while stride < device_count:
        radix = 4 if stride * 4 <= device_count else 2
        received = []
        for digit in range(1, radix):
            pairs = [(k, k ^ (digit * stride)) for k in range(device_count)]
            received.append(lax.ppermute(values, axes, pairs))
        for block in received:
            values = jnp.maximum(values, block)
        stride *= radix
    return values


def make_body(plane_count, inner_count, term_count):
    all_axes = ("plane", "inner", "term")

    def body(receptor_grids, term_weights, atom_weights, ligand_cells):
        terms_here, rows_here, cells = receptor_grids.shape
        rot_here = ligand_cells.shape[1]
        rot_total = rot_here * plane_count * inner_count
        plane = lax.axis_index("plane")
        inner = lax.axis_index("inner")
        term = lax.axis_index("term")
        own_rows = lax.all_gather(receptor_grids, "inner", axis=1, tiled=True)
        groups = gather_by_permutes(own_rows, "term", term_count, term)
        local_slots = jnp.arange(rot_here * plane_count, dtype=jnp.int32) // rot_here
        if plane_count & (plane_count - 1):
            cell_blocks = gather_by_permutes(ligand_cells, "plane", plane_count, plane)
            cells_here = jnp.concatenate(cell_blocks, axis=1)
            slot_plane = (plane - local_slots) % plane_count
        else:
            cells_here = ligand_cells
            shift = 1
            while shift < plane_count:
                pairs = [(k, k ^ shift) for k in range(plane_count)]
                moved = lax.ppermute(cells_here, "plane", pairs)
                cells_here = jnp.concatenate([cells_here, moved], axis=1)
                shift *= 2
            slot_plane = jnp.bitwise_xor(plane, local_slots)
        share = cells_here.shape[1] // term_count
        voxels = lax.dynamic_slice_in_dim(cells_here, term * share, share, axis=1)
        local = term * share + jnp.arange(share, dtype=jnp.int32)
        source_plane = lax.dynamic_slice_in_dim(slot_plane, term * share, share)
        rot_ids = (source_plane * inner_count + inner) * rot_here + local % rot_here
        coefficients = atom_weights * term_weights[:, None]
        coefficients = jnp.concatenate(gather_by_permutes(coefficients, "term", term_count, term))
        with jax.named_scope("twiddle_tables"):
            factors = plane_factors()
            table_hi, table_lo = split_bf16(plane_table(factors, G))
            box_table = plane_table(factors, LB)
            tables = lax.optimization_barrier((box_table, table_hi, table_lo))
            box_table, table_hi, table_lo = tables
        with jax.named_scope("ligand_spectra"):
            lig_spec = ligand_spectra(voxels, coefficients, box_table)
        products = 0.0
        for index, grids in enumerate(groups):
            lo = index * terms_here
            with jax.named_scope("receptor_spectra"):
                rec_spec = receptor_mixed(grids, table_hi)
            with jax.named_scope("correlate"):
                products = products + correlate(rec_spec, lig_spec[:, lo : lo + terms_here])
        with jax.named_scope("inverse_scores"):
            scores = inverse_scores(products, table_hi, table_lo)
            best_here = jnp.max(scores, axis=(2, 3))[0]
        receptors = plane_count
        columns = jnp.arange(rot_total, dtype=jnp.int32)
        hit = rot_ids[:, None] == columns[None, :]
        row = jnp.max(jnp.where(hit, best_here[:, None], -jnp.inf), axis=0)
        mine = jnp.arange(receptors, dtype=jnp.int32)[:, None] == plane
        placed = jnp.where(mine, row[None, :], -jnp.inf)
        placed = butterfly_max(placed, all_axes, plane_count * inner_count * term_count)
        start = (plane * inner_count + inner) * rot_here
        best_scores = lax.dynamic_slice_in_dim(placed, start, rot_here, axis=1)
        best_overall = jnp.max(placed, axis=1)
        return (best_scores, best_overall)

    return body


def solution(mesh):
    rot_count = mesh.shape["rot"]
    term_count = mesh.shape["term"]

    def run(receptor_grids, term_weights, atom_weights, ligand_cells):
        receptors = receptor_grids.shape[1] // G
        inner_count = rot_count // receptors
        devices = np.asarray(mesh.devices).reshape(receptors, inner_count, term_count)
        fine = jax.sharding.Mesh(devices, ("plane", "inner", "term"))
        rows = ("plane", "inner")
        placed = (P("term", rows, None), P("term"), P("term", None), P(None, rows, None))
        mapped = jax.shard_map(
            make_body(receptors, inner_count, term_count),
            mesh=fine,
            in_specs=placed,
            out_specs=(P(None, rows), P()),
            check_vma=False,
        )
        return mapped(receptor_grids, term_weights, atom_weights, ligand_cells)

    return run
```

```python
import math

import numpy as np

import jax
import jax.numpy as jnp
from jax import lax
from jax.sharding import PartitionSpec as P

G = 32
HZ = G // 2 + 1
LB = 16
WIDTH = 640

HIGH = lax.Precision.HIGH
HIGHEST = lax.Precision.HIGHEST


def line_table(freq_count, cell_count):
    freq = np.arange(freq_count)[:, None]
    cell = np.arange(cell_count)[None, :]
    phase = (freq * cell % G).astype(np.float64) * (2.0 * math.pi / G)
    return np.cos(phase).astype(np.float32), np.sin(phase).astype(np.float32)


def plane_factors():
    column = np.arange(2 * WIDTH)
    half = column // WIDTH
    freq = column % WIDTH
    valid = freq < G * HZ
    cell = np.arange(G)[:, None]
    phase_y = (cell * (freq // HZ)[None, :] % G) * (2.0 * math.pi / G)
    phase_z = (cell * (freq % HZ)[None, :] % G) * (2.0 * math.pi / G)
    cy, sy = np.cos(phase_y), np.sin(phase_y)
    cz, sz = np.cos(phase_z), np.sin(phase_z)
    first = np.where(half == 0, cy, sy) * valid
    third = np.where(half == 0, -sy, cy) * valid
    return [jnp.asarray(f.astype(np.float32)) for f in (first, cz, third, sz)]


def plane_table(factors, side):
    first, second, third, fourth = [
        jnp.transpose(f[:side].reshape(side, 2, WIDTH), (1, 0, 2)) for f in factors
    ]
    table = first[:, :, None, :] * second[:, None, :, :] + third[:, :, None, :] * fourth[:, None, :, :]
    return table.reshape(2, side * side, WIDTH)


def split_bf16(table):
    upper = lax.reduce_precision(table, exponent_bits=8, mantissa_bits=7)
    lower = table - upper
    return upper.astype(jnp.bfloat16), lower.astype(jnp.bfloat16)


def mix_tables(cell_count):
    cos_x, sin_x = line_table(G, cell_count)
    from_cos = np.concatenate([cos_x, -sin_x], axis=0)
    from_sin = np.concatenate([-sin_x, -cos_x], axis=0)
    return jnp.asarray(np.concatenate([from_cos, from_sin], axis=1))


def mix_table(cell_count):
    cos_x, sin_x = line_table(G, cell_count)
    return jnp.asarray(np.concatenate([cos_x, sin_x], axis=0))


def receptor_mixed(grids, table_hi):
    terms, rows, cells = grids.shape
    receptors = rows // G
    grids = grids.reshape(terms, receptors, G, cells)
    plane = jnp.einsum("trxc,hcq->trhxq", grids, table_hi, preferred_element_type=jnp.float32)
    plane = plane.reshape(terms, receptors, 2 * G, WIDTH)
    return jnp.einsum("pk,trkq->trpq", mix_tables(G), plane, precision=HIGH)


def ligand_spectra(voxels, coefficients, box_table):
    yz_index = voxels[1] * LB + voxels[2]
    cells = jnp.arange(LB * LB, dtype=jnp.int32)
    onehot = (yz_index[:, :, None] == cells[None, None, :]).astype(jnp.bfloat16)
    x_cells = jnp.arange(LB, dtype=jnp.int32)
    in_x = (voxels[0][:, None, :] == x_cells[None, :, None]).astype(jnp.float32)
    weights = coefficients[None, :, None, :] * in_x[:, None, :, :]
    upper, lower = split_bf16(weights)
    form = "ntxa,nac->ntxc"
    grid = jnp.einsum(form, upper, onehot, preferred_element_type=jnp.float32)
    grid = grid + jnp.einsum(form, lower, onehot, preferred_element_type=jnp.float32)
    plane = jnp.einsum("ntxc,hcq->nthxq", grid, box_table, precision=HIGH)
    rot_count, terms = plane.shape[0], plane.shape[1]
    plane = plane.reshape(rot_count, terms, 2 * LB, WIDTH)
    return jnp.einsum("pk,ntkq->tnpq", mix_tables(LB), plane, precision=HIGH)


def correlate(rec_spec, lig_spec):
    rr = rec_spec[:, :, None, :G]
    ri = rec_spec[:, :, None, G:]
    lr = lig_spec[:, None, :, :G]
    li = lig_spec[:, None, :, G:]
    prod_re = jnp.sum(lr * rr + li * ri, axis=0)
    prod_im = jnp.sum(lr * ri - li * rr, axis=0)
    return jnp.stack([prod_re, prod_im], axis=0)


def inverse_scores(products, table_hi, table_lo):
    mixed = jnp.einsum("xp,srnpq->srnxq", mix_table(G), products, precision=HIGH)
    inv_re = mixed[0, :, :, :G] - mixed[1, :, :, G:]
    inv_im = mixed[1, :, :, :G] + mixed[0, :, :, G:]
    column = np.arange(WIDTH)
    freq_z = column % HZ
    fold = np.where((freq_z == 0) | (freq_z == G // 2), 1.0, 2.0) / float(G**3)
    fold = np.where(column < G * HZ, fold, 0.0)
    fold = jnp.asarray(fold.astype(np.float32))
    joined = jnp.stack([inv_re * fold, -inv_im * fold], axis=3)
    upper, lower = lax.optimization_barrier(split_bf16(joined))
    form = "rnxhq,hcq->rnxc"
    scores = jnp.einsum(form, upper, table_hi, preferred_element_type=jnp.float32)
    scores = scores + jnp.einsum(form, lower, table_hi, preferred_element_type=jnp.float32)
    return scores + jnp.einsum(form, upper, table_lo, preferred_element_type=jnp.float32)


def gather_by_permutes(values, axis_name, count, here):
    blocks = [values]
    for shift in range(1, count):
        pairs = [(k, (k + shift) % count) for k in range(count)]
        blocks.append(lax.ppermute(values, axis_name, pairs))
    return blocks


def butterfly_max(values, axes, device_count):
    stride = 1
    while stride < device_count:
        radix = 4 if stride > 1 and stride * 4 <= device_count else 2
        received = []
        for digit in range(1, radix):
            pairs = [(k, k ^ (digit * stride)) for k in range(device_count)]
            received.append(lax.ppermute(values, axes, pairs))
        for block in received:
            values = jnp.maximum(values, block)
        stride *= radix
    return values


def make_body(plane_count, inner_count, term_count):
    all_axes = ("plane", "inner", "term")

    def body(receptor_grids, term_weights, atom_weights, ligand_cells):
        terms_here, rows_here, cells = receptor_grids.shape
        rot_here = ligand_cells.shape[1]
        rot_total = rot_here * plane_count * inner_count
        plane = lax.axis_index("plane")
        inner = lax.axis_index("inner")
        term = lax.axis_index("term")
        own_rows = lax.all_gather(receptor_grids, "inner", axis=1, tiled=True)
        groups = gather_by_permutes(own_rows, "term", term_count, term)
        local_slots = jnp.arange(rot_here * plane_count, dtype=jnp.int32) // rot_here
        if plane_count & (plane_count - 1):
            cell_blocks = gather_by_permutes(ligand_cells, "plane", plane_count, plane)
            cells_here = jnp.concatenate(cell_blocks, axis=1)
            slot_plane = (plane - local_slots) % plane_count
        else:
            cells_here = ligand_cells
            shift = 1
            while shift < plane_count:
                pairs = [(k, k ^ shift) for k in range(plane_count)]
                moved = lax.ppermute(cells_here, "plane", pairs)
                cells_here = jnp.concatenate([cells_here, moved], axis=1)
                shift *= 2
            slot_plane = jnp.bitwise_xor(plane, local_slots)
        share = cells_here.shape[1] // term_count
        voxels = lax.dynamic_slice_in_dim(cells_here, term * share, share, axis=1)
        local = term * share + jnp.arange(share, dtype=jnp.int32)
        source_plane = lax.dynamic_slice_in_dim(slot_plane, term * share, share)
        rot_ids = (source_plane * inner_count + inner) * rot_here + local % rot_here
        coefficients = atom_weights * term_weights[:, None]
        coefficients = jnp.concatenate(gather_by_permutes(coefficients, "term", term_count, term))
        with jax.named_scope("twiddle_tables"):
            factors = plane_factors()
            table_hi, table_lo = split_bf16(plane_table(factors, G))
            box_table = plane_table(factors, LB)
            tables = lax.optimization_barrier((box_table, table_hi, table_lo))
            box_table, table_hi, table_lo = tables
        with jax.named_scope("ligand_spectra"):
            lig_spec = ligand_spectra(voxels, coefficients, box_table)
        products = 0.0
        for index, grids in enumerate(groups):
            lo = index * terms_here
            with jax.named_scope("receptor_spectra"):
                rec_spec = receptor_mixed(grids, table_hi)
            with jax.named_scope("correlate"):
                products = products + correlate(rec_spec, lig_spec[lo : lo + terms_here])
        with jax.named_scope("inverse_scores"):
            scores = inverse_scores(products, table_hi, table_lo)
            best_here = jnp.max(scores, axis=(2, 3))[0]
        receptors = plane_count
        columns = jnp.arange(rot_total, dtype=jnp.int32)
        hit = rot_ids[:, None] == columns[None, :]
        row = jnp.max(jnp.where(hit, best_here[:, None], -jnp.inf), axis=0)
        mine = jnp.arange(receptors, dtype=jnp.int32)[:, None] == plane
        placed = jnp.where(mine, row[None, :], -jnp.inf)
        placed = butterfly_max(placed, all_axes, plane_count * inner_count * term_count)
        start = (plane * inner_count + inner) * rot_here
        best_scores = lax.dynamic_slice_in_dim(placed, start, rot_here, axis=1)
        best_overall = jnp.max(placed, axis=1)
        return (best_scores, best_overall)

    return body


def solution(mesh):
    rot_count = mesh.shape["rot"]
    term_count = mesh.shape["term"]

    def run(receptor_grids, term_weights, atom_weights, ligand_cells):
        receptors = receptor_grids.shape[1] // G
        inner_count = rot_count // receptors
        devices = np.asarray(mesh.devices).reshape(receptors, inner_count, term_count)
        fine = jax.sharding.Mesh(devices, ("plane", "inner", "term"))
        rows = ("plane", "inner")
        placed = (P("term", rows, None), P("term"), P("term", None), P(None, rows, None))
        mapped = jax.shard_map(
            make_body(receptors, inner_count, term_count),
            mesh=fine,
            in_specs=placed,
            out_specs=(P(None, rows), P()),
            check_vma=False,
        )
        return mapped(receptor_grids, term_weights, atom_weights, ligand_cells)

    return run
```
